128 devices in a mesh: segment: 4 (over x), dp: 32 (over y, z, core).
Axes of the slice: x: 4, y: 4, z: 4, core: 2. Of those that a mesh axis runs over, the one named last changes fastest.
Arguments:
- query_states: bfloat16 [1024, 32, 768], P('dp'), may hold values from -40 to 40
- passage_states: bfloat16 [512, 64, 768], P('dp'), may hold values from -40 to 40
- query_tokens: int32 [1024, 32], P('dp'), may hold values from 0 to 32099, as said below
- passage_tokens: int32 [512, 64], P('dp'), may hold values from 0 to 32099, as said below
- ff_gains: float32 [2, 768], replicated, may hold values from 0.1 to 1.9
- out_gains: float32 [2, 768], replicated, may hold values from 0.1 to 1.9
- w_gate: bfloat16 [2, 768, 2048], P(None, None, 'segment'), may hold values from -0.21875 to 0.21875
- w_up: bfloat16 [2, 768, 2048], P(None, None, 'segment'), may hold values from -0.21875 to 0.21875
- w_down: bfloat16 [2, 2048, 768], P(None, 'segment'), may hold values from -1 to 1
- w_proj: bfloat16 [2, 768, 768], replicated, may hold values from -0.21875 to 0.21875
- positive_ids: int32 [1024], P('dp'), may hold values from 0 to 511
- negative_ids: int32 [1024, 15], P('dp'), may hold values from 0 to 511
- negative_counts: int32 [1024], P('dp'), may hold values from 1 to 15, 7680 in all
Outputs:
- grad_gate: float32 [2, 768, 2048], P(None, 'dp', 'segment')
- grad_up: float32 [2, 768, 2048], P(None, 'dp', 'segment')
- grad_down: float32 [2, 2048, 768], P(None, 'segment', 'dp')
The draws below stay inside these ranges and needn't reach their ends.
Inputs may be any that keep to these rules, and one draw needn't show every extreme that they name: `query_tokens`: each row holds token ids of 1 or more followed by zeros, at least 8 nonzero ids; the first row has no zeros. `passage_tokens`: each row holds token ids of 1 or more followed by zeros, at least 16 nonzero ids; the first row has no zeros. Only the first negative_counts[i] entries of row i are used; the counts sum to 7680.
All inputs are finite; a program needn't handle non-finite values. No bound on the sum of `negative_counts` on one device may be relied on, other than what follows from the above.
Results may differ from the reference program's by a relative error of at most 0.012.
Values may be sent and summed in bfloat16 or wider, within the bound.
No kernel may reach another device: no remote copies, remote signals or barrier semaphores. Data moves between devices by JAX's collectives and lax.ppermute only.
A program may use at most 128 MiB of HBM per device.

```python
import math
import jax
import jax.numpy as jnp
import numpy as np
from jax import lax

D = 768
FF = 2048
QLEN = 32
PLEN = 64
NEG_MAX = 15
QUERIES = 1024
PASSAGES = 512


def token_rows(key, row_count, length):
    length_key, word_key = jax.random.split(key)
    lengths = jax.random.randint(length_key, (row_count, 1), length // 4, length + 1)
    lengths = jnp.where(jnp.arange(row_count)[:, None] == 0, length, lengths)
    token_words = jax.random.randint(word_key, (row_count, length), 1, 32100)
    return jnp.where(jnp.arange(length)[None, :] < lengths, token_words, 0).astype(jnp.int32)


def state_rows(key, row_count, length):
    subkeys = jax.random.split(key, 3)
    noise = jnp.clip(jax.random.normal(subkeys[0], (row_count, length, D)), -4.0, 4.0)
    column_low = math.log(0.3)
    column_high = math.log(3.0)
    row_low = math.log(0.05)
    row_high = math.log(0.5)
    columns = jnp.exp(jax.random.uniform(subkeys[1], (D,), minval=column_low, maxval=column_high))
    row_scale = jnp.exp(jax.random.uniform(subkeys[2], (row_count, length, 1), minval=row_low, maxval=row_high))
    position = jnp.arange(row_count).astype(jnp.float32) / max(row_count - 1, 1)
    trend = jnp.exp(math.log(4.0) * position)[:, None, None]
    return jnp.clip(noise * columns * row_scale * trend, -40.0, 40.0).astype(jnp.bfloat16)


def draw_query_states(key, part):
    return state_rows(key, QUERIES, QLEN)


def draw_passage_states(key, part):
    return state_rows(key, PASSAGES, PLEN)


def draw_query_tokens(key, part):
    return token_rows(key, QUERIES, QLEN)


def draw_passage_tokens(key, part):
    return token_rows(key, PASSAGES, PLEN)


def draw_w_down(key, part):
    noise_key, column_key = jax.random.split(key, 2)
    noise = jnp.clip(jax.random.normal(noise_key, (2, FF, D)), -4.0, 4.0)
    shared = jnp.clip(jax.random.normal(column_key, (2, 1, D)), -3.0, 3.0)
    strength = 1.2
    return ((noise + strength * shared) / math.sqrt(FF)).astype(jnp.bfloat16)


def place_ends(array, key, smallest, high):
    longest = array.shape.index(max(array.shape))
    spots = []
    for shift in (0, 1):
        where = [jax.random.randint(jax.random.fold_in(key, axis), (), 0, length) for axis, length in enumerate(array.shape)]
        where[longest] = (where[longest] + shift) % array.shape[longest]
        spots.append(tuple(where))
    return array.at[spots[0]].set(smallest).at[spots[1]].set(high)


def shard_levels(stream_key, extent, cuts, smallest, top_value):
    def one(axis_at, shards_of):
        draws = jax.random.uniform(jax.random.fold_in(jax.random.fold_in(stream_key, 6), axis_at), (shards_of,), jnp.float32, smallest / len(cuts), top_value / len(cuts))
        return jnp.repeat(jnp.exp(draws), extent[axis_at] // shards_of).reshape((-1,) + (1,) * (len(extent) - axis_at - 1))

    loudness = one(*cuts[0])
    for cut in cuts[1:]:
        loudness = loudness * one(*cut)
    return loudness


def length_profile(number_of, total, most, skew):
    loads = [(1 << 20) // math.isqrt(rank ** skew) + 1 for rank in range(2, number_of + 1)]
    rest, given = total - most - (number_of - 1), [1] * (number_of - 1)
    while rest > 0:
        candidates = [i for i in range(number_of - 1) if given[i] < most]
        mass, budget = sum([loads[i] for i in candidates]), rest
        for i in candidates:
            addition = min(most - given[i], max(1, budget * loads[i] // mass), rest)
            given[i] = given[i] + addition
            rest = rest - addition
    return np.array([most] + given)


def ragged(own_key, amount, total, bound, lean):
    if amount == 2:
        one = jax.random.randint(own_key, (), max(1, total - bound), min(bound, total - 1) + 1)
        return jnp.stack([one, total - one])
    sizes = jnp.asarray(length_profile(amount, total, bound, lean), jnp.int32)
    couples = (amount - 1) // 2
    giver, sink = sizes[1:1 + 2 * couples:2], sizes[2:2 + 2 * couples:2]
    margin = jnp.minimum(giver - 1, bound - sink)
    shifted = jax.random.randint(jax.random.fold_in(own_key, 1), (couples,), 0, 1 << 20) % (margin + 1)
    sizes = sizes.at[1:1 + 2 * couples:2].set(giver - shifted).at[2:2 + 2 * couples:2].set(sink + shifted)
    return sizes[jax.random.permutation(jax.random.fold_in(own_key, 2), amount)]


def scatter_about(rng, shape, spread, limit, cuts=(), held_as=jnp.bfloat16):
    array = spread * jax.random.normal(rng, shape, jnp.float32)
    if cuts:
        array = array * shard_levels(rng, shape, cuts, -0.22, 0.18)
    return jnp.clip(array, -limit, limit).astype(held_as)


def setup_inputs(seed: int = 0) -> dict:
    streams_of = jax.random.split(jax.random.key(seed), 14)
    return {
        "query_states": draw_query_states(jax.random.fold_in(streams_of[13], 71), 0),
        "passage_states": draw_passage_states(jax.random.fold_in(streams_of[13], 71), 0),
        "query_tokens": draw_query_tokens(jax.random.fold_in(streams_of[13], 71), 0),
        "passage_tokens": draw_passage_tokens(jax.random.fold_in(streams_of[13], 71), 0),
        "ff_gains": jnp.clip(1.0 + 0.18 * jax.random.normal(streams_of[4], (2, D), jnp.float32), 0.1, 1.9),
        "out_gains": jnp.clip(1.0 + 0.18 * jax.random.normal(streams_of[5], (2, D), jnp.float32), 0.1, 1.9),
        "w_gate": scatter_about(streams_of[6], (2, D, FF), D ** -0.5, 0.21875, ((2, 4),)),
        "w_up": scatter_about(streams_of[7], (2, D, FF), D ** -0.5, 0.21875, ((2, 4),)),
        "w_down": draw_w_down(jax.random.fold_in(streams_of[13], 71), 0),
        "w_proj": scatter_about(streams_of[9], (2, D, D), D ** -0.5, 0.21875),
        "positive_ids": place_ends(jax.random.randint(streams_of[10], (QUERIES,), 0, PASSAGES), jax.random.fold_in(streams_of[10], 1), 0, PASSAGES - 1).astype(jnp.int32),
        "negative_ids": place_ends(jax.random.randint(streams_of[11], (QUERIES, NEG_MAX), 0, PASSAGES), jax.random.fold_in(streams_of[11], 1), 0, PASSAGES - 1).astype(jnp.int32),
        "negative_counts": ragged(streams_of[12], QUERIES, QUERIES * NEG_MAX // 2, NEG_MAX, 2).astype(jnp.int32),
    }


score_temp = 0.05
rank_temp = 1.0
recall_depth = 5.0
loss_scale = 16.0
norm_eps = 1e-06
block_rows = 16

def inverse_rms(values):
    return lax.rsqrt(lax.optimization_barrier(jnp.mean(values * values, axis=-1, keepdims=True)) + norm_eps)

def normed_input(states, ff_gain):
    widened = states.astype(jnp.float32)
    return (widened * inverse_rms(widened) * ff_gain).astype(jnp.bfloat16)

def pooled_embedding(summed, tokens, out_gain, proj_weight):
    normed = summed * inverse_rms(summed) * out_gain
    token_mask = (tokens != 0).astype(jnp.float32)[:, :, None]
    pooled = lax.optimization_barrier(jnp.sum(normed * token_mask, axis=1)) / lax.optimization_barrier(jnp.sum(token_mask, axis=1))
    projected = jnp.dot(pooled, proj_weight.astype(jnp.float32), precision=lax.Precision.HIGHEST)
    return projected * lax.rsqrt(lax.optimization_barrier(jnp.sum(projected * projected, axis=-1, keepdims=True)) + norm_eps)

def recall_loss(scores, valid_mask):
    margins = (scores[:, 1:] - scores[:, :1]) / score_temp
    soft_ranks = 1.0 + lax.optimization_barrier(jnp.sum(jax.nn.sigmoid(margins) * valid_mask, axis=1))
    return loss_scale * jnp.sum(jax.nn.sigmoid((soft_ranks - recall_depth - 0.5) / rank_temp))

def tower_forward(states, ff_gain, gate_weight, up_weight, down_weight):
    model_width = states.shape[-1]

    def one_block(row_block):
        normed = normed_input(row_block, ff_gain).reshape(-1, model_width)
        gate_pre = jnp.dot(normed, gate_weight, preferred_element_type=jnp.float32)
        up_pre = jnp.dot(normed, up_weight, preferred_element_type=jnp.float32)
        hidden = (jax.nn.gelu(gate_pre) * up_pre).astype(jnp.bfloat16)
        branch = jnp.dot(hidden, down_weight, preferred_element_type=jnp.float32)
        return row_block.astype(jnp.float32) + branch.reshape(row_block.shape)
    blocks = states.reshape((-1, block_rows) + states.shape[1:])
    return lax.map(one_block, blocks).reshape(states.shape)

def tower_grads(states, row_grads, ff_gain, gate_weight, up_weight, down_weight):
    model_width = states.shape[-1]

    def one_block(totals, block_pair):
        row_block, cotangent = block_pair
        normed = normed_input(row_block, ff_gain).reshape(-1, model_width)
        gate_pre = jnp.dot(normed, gate_weight, preferred_element_type=jnp.float32)
        up_pre = jnp.dot(normed, up_weight, preferred_element_type=jnp.float32)
        activated, gelu_back = jax.vjp(jax.nn.gelu, gate_pre)
        hidden = (activated * up_pre).astype(jnp.bfloat16)
        flat_grad = cotangent.reshape(-1, model_width)
        hidden_grad = jnp.dot(flat_grad, down_weight.T, preferred_element_type=jnp.float32)
        gate_grad = gelu_back(hidden_grad * up_pre)[0].astype(jnp.bfloat16)
        up_grad = (hidden_grad * activated).astype(jnp.bfloat16)
        return ((totals[0] + jnp.dot(normed.T, gate_grad, preferred_element_type=jnp.float32), totals[1] + jnp.dot(normed.T, up_grad, preferred_element_type=jnp.float32), totals[2] + jnp.dot(hidden.T, flat_grad, preferred_element_type=jnp.float32)), None)
    hidden_units = gate_weight.shape[1]
    initial = (jnp.zeros((model_width, hidden_units), jnp.float32), jnp.zeros((model_width, hidden_units), jnp.float32), jnp.zeros((hidden_units, model_width), jnp.float32))
    blocks = states.reshape((-1, block_rows) + states.shape[1:])
    grad_blocks = row_grads.reshape((-1, block_rows) + row_grads.shape[1:])
    totals, unused = lax.scan(one_block, initial, (blocks, grad_blocks))
    return totals

def reference(query_states, passage_states, query_tokens, passage_tokens, ff_gains, out_gains, w_gate, w_up, w_down, w_proj, positive_ids, negative_ids, negative_counts):
    query_sum = tower_forward(query_states, ff_gains[0], w_gate[0], w_up[0], w_down[0])
    passage_sum = tower_forward(passage_states, ff_gains[1], w_gate[1], w_up[1], w_down[1])
    query_embed, query_back = jax.vjp(lambda summed: pooled_embedding(summed, query_tokens, out_gains[0], w_proj[0]), query_sum)
    passage_embed, passage_back = jax.vjp(lambda summed: pooled_embedding(summed, passage_tokens, out_gains[1], w_proj[1]), passage_sum)
    query_round = query_embed.astype(jnp.bfloat16)
    passage_round = passage_embed.astype(jnp.bfloat16)
    cand_ids = jnp.concatenate([positive_ids[:, None], negative_ids], axis=1).astype(jnp.int32)
    cand_rows = passage_round[cand_ids].astype(jnp.float32)
    scores = jnp.einsum('qd,qcd->qc', query_round.astype(jnp.float32), cand_rows, precision=lax.Precision.HIGHEST)
    slots = negative_ids.shape[1]
    valid_mask = (lax.broadcasted_iota(jnp.int32, (negative_ids.shape[0], slots), 1) < negative_counts[:, None]).astype(jnp.float32)
    score_grads = jax.grad(recall_loss)(scores, valid_mask)
    query_grad = jnp.einsum('qc,qcd->qd', score_grads, cand_rows, precision=lax.Precision.HIGHEST)
    model_width = query_states.shape[-1]
    terms = (score_grads[:, :, None] * query_round.astype(jnp.float32)[:, None, :]).reshape(-1, model_width)
    passage_grad = jnp.zeros((passage_states.shape[0], model_width), jnp.float32).at[cand_ids.reshape(-1)].add(terms)
    query_rows = query_back(query_grad)[0].astype(jnp.bfloat16)
    passage_rows = passage_back(passage_grad)[0].astype(jnp.bfloat16)
    query_grads = tower_grads(query_states, query_rows, ff_gains[0], w_gate[0], w_up[0], w_down[0])
    passage_grads = tower_grads(passage_states, passage_rows, ff_gains[1], w_gate[1], w_up[1], w_down[1])
    return (jnp.stack([query_grads[0], passage_grads[0]]), jnp.stack([query_grads[1], passage_grads[1]]), jnp.stack([query_grads[2], passage_grads[2]]))
```

```python
import jax
import jax.numpy as jnp
from jax import lax
from jax.sharding import PartitionSpec as P

score_temp = 0.05
rank_temp = 1.0
recall_depth = 5.0
loss_scale = 16.0
norm_eps = 1e-06


def inverse_rms(values):
    return lax.rsqrt(jnp.mean(values * values, axis=-1, keepdims=True) + norm_eps)


def normed_input(states, ff_gain):
    widened = states.astype(jnp.float32)
    return (widened * inverse_rms(widened) * ff_gain).astype(jnp.bfloat16)


def pooled_embedding(summed, tokens, out_gain, proj_weight):
    normed = summed * inverse_rms(summed) * out_gain
    token_mask = (tokens != 0).astype(jnp.float32)[:, :, None]
    pooled = jnp.sum(normed * token_mask, axis=1) / jnp.sum(token_mask, axis=1)
    projected = jnp.dot(pooled, proj_weight.astype(jnp.float32), precision=lax.Precision.HIGHEST)
    return projected * lax.rsqrt(jnp.sum(projected * projected, axis=-1, keepdims=True) + norm_eps)


def recall_loss(scores, valid_mask):
    margins = (scores[:, 1:] - scores[:, :1]) / score_temp
    soft_ranks = 1.0 + jnp.sum(jax.nn.sigmoid(margins) * valid_mask, axis=1)
    return loss_scale * jnp.sum(jax.nn.sigmoid((soft_ranks - recall_depth - 0.5) / rank_temp))


def contract(left, right):
    return lax.dot_general(
        left, right, (((0,), (0,)), ((), ())), preferred_element_type=jnp.float32
    )


def natural_order(gathered, segments, groups, per_device):
    model_width = gathered.shape[-1]
    shaped = gathered.reshape(segments, groups, per_device, model_width)
    return jnp.transpose(shaped, (1, 0, 2, 3)).reshape(-1, model_width)


def score_grads_of(scores, counts):
    slots = scores.shape[1] - 1
    valid_mask = (
        lax.broadcasted_iota(jnp.int32, (scores.shape[0], slots), 1) < counts[:, None]
    ).astype(jnp.float32)
    return jax.grad(recall_loss)(scores, valid_mask)


def body(
    query_states,
    passage_states,
    query_tokens,
    passage_tokens,
    ff_gains,
    out_gains,
    w_gate,
    w_up,
    w_down,
    w_proj,
    positive_ids,
    negative_ids,
    negative_counts,
):
    segments = lax.axis_size("segment")
    groups = lax.axis_size("dp")
    segment_index = lax.axis_index("segment")
    model_width = query_states.shape[-1]
    query_dev = query_states.shape[0] // segments
    passage_dev = passage_states.shape[0] // segments

    def forward_part(states, tower_index):
        normed = normed_input(states, ff_gains[tower_index]).reshape(-1, model_width)
        gate_pre = jnp.dot(normed, w_gate[tower_index], preferred_element_type=jnp.float32)
        up_pre = jnp.dot(normed, w_up[tower_index], preferred_element_type=jnp.float32)
        activated, gelu_back = jax.vjp(jax.nn.gelu, gate_pre)
        hidden = (activated * up_pre).astype(jnp.bfloat16)
        branch = jnp.dot(hidden, w_down[tower_index], preferred_element_type=jnp.float32).reshape(
            states.shape
        )
        return (normed, up_pre, activated, gelu_back, hidden, branch)

    def own_rows(values, per_device):
        return lax.dynamic_slice_in_dim(values, segment_index * per_device, per_device, 0)

    def head_of(tokens, tower_index):
        return lambda summed: pooled_embedding(
            summed, tokens, out_gains[tower_index], w_proj[tower_index]
        )

    query_parts = forward_part(query_states, 0)
    passage_parts = forward_part(passage_states, 1)
    query_branch, passage_branch = (
        lax.psum_scatter(query_parts[5], "segment", scatter_dimension=0, tiled=True),
        lax.psum_scatter(passage_parts[5], "segment", scatter_dimension=0, tiled=True),
    )
    query_embed, query_back = jax.vjp(
        head_of(own_rows(query_tokens, query_dev), 0),
        own_rows(query_states, query_dev).astype(jnp.float32) + query_branch,
    )
    passage_embed, passage_back = jax.vjp(
        head_of(own_rows(passage_tokens, passage_dev), 1),
        own_rows(passage_states, passage_dev).astype(jnp.float32) + passage_branch,
    )
    query_round = query_embed.astype(jnp.bfloat16)
    passage_round = passage_embed.astype(jnp.bfloat16)
    passage_group = lax.all_gather(passage_round, "segment", axis=0, tiled=True)
    passage_all = lax.all_gather(passage_group, "dp", axis=0, tiled=True)
    cand_ids = jnp.concatenate(
        [own_rows(positive_ids, query_dev)[:, None], own_rows(negative_ids, query_dev)], axis=1
    )
    cand_rows = passage_all[cand_ids]
    scores = jnp.einsum("qd,qcd->qc", query_round, cand_rows, preferred_element_type=jnp.float32)
    score_grads = score_grads_of(scores, own_rows(negative_counts, query_dev))
    query_grad = jnp.einsum(
        "qc,qcd->qd", score_grads, cand_rows.astype(jnp.float32), precision=lax.Precision.HIGHEST
    )
    passage_total = passage_all.shape[0]
    every_id = lax.broadcasted_iota(jnp.int32, (1, 1, passage_total), 2)
    matches = (cand_ids[:, :, None] == every_id).astype(jnp.float32)
    coefficient = jnp.einsum("qcp,qc->pq", matches, score_grads, precision=lax.Precision.HIGHEST)
    natural_grads = jnp.dot(
        coefficient, query_round.astype(jnp.float32), precision=lax.Precision.HIGHEST
    )
    group_grads = lax.psum_scatter(natural_grads, "dp", scatter_dimension=0, tiled=True)
    passage_grad = lax.psum_scatter(group_grads, "segment", scatter_dimension=0, tiled=True)
    query_share = query_back(query_grad)[0].astype(jnp.bfloat16)
    passage_share = passage_back(passage_grad)[0].astype(jnp.bfloat16)
    query_rows, passage_rows = (
        lax.all_gather(query_share, "segment", axis=0, tiled=True),
        lax.all_gather(passage_share, "segment", axis=0, tiled=True),
    )

    def backward_part(tower_parts, row_grads, tower_index):
        normed, up_pre, activated, gelu_back, hidden, branch = tower_parts
        flat_grad = row_grads.reshape(-1, model_width)
        hidden_grad = lax.dot_general(
            flat_grad,
            w_down[tower_index],
            (((1,), (1,)), ((), ())),
            preferred_element_type=jnp.float32,
        )
        gate_grad = gelu_back(hidden_grad * up_pre)[0].astype(jnp.bfloat16)
        up_grad = (hidden_grad * activated).astype(jnp.bfloat16)
        return (normed, gate_grad, up_grad, hidden, flat_grad)

    towers_back = (
        backward_part(query_parts, query_rows, 0),
        backward_part(passage_parts, passage_rows, 1),
    )

    def weight_terms():
        matrices = [[], [], []]
        for normed, gate_grad, up_grad, hidden, flat_grad in towers_back:
            matrices[0].append(contract(normed, gate_grad))
            matrices[1].append(contract(normed, up_grad))
            matrices[2].append(contract(flat_grad, hidden))
        return jnp.stack([jnp.stack(pieces, axis=1) for pieces in matrices], axis=1)

    summed_grads = lax.psum_scatter(weight_terms(), "dp", scatter_dimension=0, tiled=True)
    grad_gate = jnp.transpose(summed_grads[:, 0], (1, 0, 2))
    grad_up = jnp.transpose(summed_grads[:, 1], (1, 0, 2))
    grad_down = jnp.transpose(summed_grads[:, 2], (1, 2, 0))
    return (grad_gate, grad_up, grad_down)


def solution(mesh):
    return jax.shard_map(
        body,
        mesh=mesh,
        in_specs=(
            P("dp", None, None),
            P("dp", None, None),
            P("dp", None),
            P("dp", None),
            P(),
            P(),
            P(None, None, "segment"),
            P(None, None, "segment"),
            P(None, "segment", None),
            P(),
            P("dp"),
            P("dp", None),
            P("dp"),
        ),
        out_specs=(P(None, "dp", "segment"), P(None, "dp", "segment"), P(None, "segment", "dp")),
        check_vma=False,
    )
```

```python
import jax
import jax.numpy as jnp
from jax import lax
from jax.sharding import PartitionSpec as P

score_temp = 0.05
rank_temp = 1.0
recall_depth = 5.0
loss_scale = 16.0
norm_eps = 1e-06


def inverse_rms(values):
    return lax.rsqrt(jnp.mean(values * values, axis=-1, keepdims=True) + norm_eps)


def normed_input(states, ff_gain):
    widened = states.astype(jnp.float32)
    return (widened * inverse_rms(widened) * ff_gain).astype(jnp.bfloat16)


def pooled_embedding(summed, tokens, out_gain, proj_weight):
    normed = summed * inverse_rms(summed) * out_gain
    token_mask = (tokens != 0).astype(jnp.float32)[:, :, None]
    pooled = jnp.sum(normed * token_mask, axis=1) / jnp.sum(token_mask, axis=1)
    projected = jnp.dot(pooled, proj_weight.astype(jnp.float32), precision=lax.Precision.HIGHEST)
    return projected * lax.rsqrt(jnp.sum(projected * projected, axis=-1, keepdims=True) + norm_eps)


def recall_loss(scores, valid_mask):
    margins = (scores[:, 1:] - scores[:, :1]) / score_temp
    soft_ranks = 1.0 + jnp.sum(jax.nn.sigmoid(margins) * valid_mask, axis=1)
    return loss_scale * jnp.sum(jax.nn.sigmoid((soft_ranks - recall_depth - 0.5) / rank_temp))


def contract(left, right):
    return lax.dot_general(
        left, right, (((0,), (0,)), ((), ())), preferred_element_type=jnp.float32
    )


def natural_order(gathered, segments, groups, per_device):
    model_width = gathered.shape[-1]
    shaped = gathered.reshape(segments, groups, per_device, model_width)
    return jnp.transpose(shaped, (1, 0, 2, 3)).reshape(-1, model_width)


def score_grads_of(scores, counts):
    slots = scores.shape[1] - 1
    valid_mask = (
        lax.broadcasted_iota(jnp.int32, (scores.shape[0], slots), 1) < counts[:, None]
    ).astype(jnp.float32)
    return jax.grad(recall_loss)(scores, valid_mask)


def body(
    query_states,
    passage_states,
    query_tokens,
    passage_tokens,
    ff_gains,
    out_gains,
    w_gate,
    w_up,
    w_down,
    w_proj,
    positive_ids,
    negative_ids,
    negative_counts,
):
    segments = lax.axis_size("segment")
    groups = lax.axis_size("dp")
    segment_index = lax.axis_index("segment")
    model_width = query_states.shape[-1]
    query_dev = query_states.shape[0] // segments
    passage_dev = passage_states.shape[0] // segments

    def forward_part(states, tower_index):
        normed = normed_input(states, ff_gains[tower_index]).reshape(-1, model_width)
        gate_pre = jnp.dot(normed, w_gate[tower_index], preferred_element_type=jnp.float32)
        up_pre = jnp.dot(normed, w_up[tower_index], preferred_element_type=jnp.float32)
        activated, gelu_back = jax.vjp(jax.nn.gelu, gate_pre)
        hidden = (activated * up_pre).astype(jnp.bfloat16)
        branch = jnp.dot(hidden, w_down[tower_index], preferred_element_type=jnp.float32).reshape(
            states.shape
        )
        return (normed, up_pre, activated, gelu_back, hidden, branch)

    def own_rows(values, per_device):
        return lax.dynamic_slice_in_dim(values, segment_index * per_device, per_device, 0)

    def head_of(tokens, tower_index):
        return lambda summed: pooled_embedding(
            summed, tokens, out_gains[tower_index], w_proj[tower_index]
        )

    query_parts = forward_part(query_states, 0)
    passage_parts = forward_part(passage_states, 1)
    query_branch, passage_branch = (
        lax.psum_scatter(query_parts[5], "segment", scatter_dimension=0, tiled=True),
        lax.psum_scatter(passage_parts[5], "segment", scatter_dimension=0, tiled=True),
    )
    query_embed, query_back = jax.vjp(
        head_of(own_rows(query_tokens, query_dev), 0),
        own_rows(query_states, query_dev).astype(jnp.float32) + query_branch,
    )
    passage_embed, passage_back = jax.vjp(
        head_of(own_rows(passage_tokens, passage_dev), 1),
        own_rows(passage_states, passage_dev).astype(jnp.float32) + passage_branch,
    )
    query_round = query_embed.astype(jnp.bfloat16)
    passage_round = passage_embed.astype(jnp.bfloat16)
    id_radix = 256
    own_ids = jnp.concatenate(
        [own_rows(positive_ids, query_dev)[:, None], own_rows(negative_ids, query_dev)], axis=1
    )
    slots = own_ids.shape[1]
    own_meta = jnp.concatenate(
        [own_ids // id_radix, own_ids % id_radix, own_rows(negative_counts, query_dev)[:, None]],
        axis=1,
    ).astype(jnp.bfloat16)
    meta_width = own_meta.shape[1]
    meta_rows = -(-query_dev * meta_width // model_width)
    meta_flat = jnp.pad(
        own_meta.reshape(-1), (0, meta_rows * model_width - query_dev * meta_width)
    ).reshape(meta_rows, model_width)
    packed = jnp.concatenate([query_round, passage_round, meta_flat], axis=0)
    gathered = lax.all_gather(packed, ("dp", "segment"), axis=0, tiled=False)
    gathered = gathered.reshape(groups, segments, -1, model_width)
    query_all = gathered[:, :, :query_dev].reshape(-1, model_width)
    passage_all = gathered[:, :, query_dev : query_dev + passage_dev].reshape(-1, model_width)
    meta_all = (
        gathered[:, :, query_dev + passage_dev :]
        .reshape(groups, segments, -1)[:, :, : query_dev * meta_width]
        .reshape(-1, meta_width)
        .astype(jnp.int32)
    )
    cand_all = meta_all[:, :slots] * id_radix + meta_all[:, slots : 2 * slots]
    counts_all = meta_all[:, 2 * slots]
    passage_total = passage_all.shape[0]
    all_scores = lax.dot_general(
        query_all, passage_all, (((1,), (1,)), ((), ())), preferred_element_type=jnp.float32
    )
    every_id = lax.broadcasted_iota(jnp.int32, (1, 1, passage_total), 2)
    matches = cand_all[:, :, None] == every_id
    scores = jnp.sum(jnp.where(matches, all_scores[:, None, :], 0.0), axis=2)
    score_grads = score_grads_of(scores, counts_all)
    coefficient = jnp.sum(jnp.where(matches, score_grads[:, :, None], 0.0), axis=1)
    dp_index = lax.axis_index("dp")
    query_start = (dp_index * segments + segment_index) * query_dev
    passage_start = (dp_index * segments + segment_index) * passage_dev
    query_coef = lax.dynamic_slice_in_dim(coefficient, query_start, query_dev, 0)
    passage_coef = lax.dynamic_slice_in_dim(coefficient, passage_start, passage_dev, 1)
    query_grad = jnp.dot(
        query_coef, passage_all.astype(jnp.float32), precision=lax.Precision.HIGHEST
    )
    passage_grad = lax.dot_general(
        passage_coef,
        query_all.astype(jnp.float32),
        (((0,), (0,)), ((), ())),
        precision=lax.Precision.HIGHEST,
        preferred_element_type=jnp.float32,
    )
    query_share = query_back(query_grad)[0].astype(jnp.bfloat16)
    passage_share = passage_back(passage_grad)[0].astype(jnp.bfloat16)
    query_rows, passage_rows = (
        lax.all_gather(query_share, "segment", axis=0, tiled=True),
        lax.all_gather(passage_share, "segment", axis=0, tiled=True),
    )

    def backward_part(tower_parts, row_grads, tower_index):
        normed, up_pre, activated, gelu_back, hidden, branch = tower_parts
        flat_grad = row_grads.reshape(-1, model_width)
        hidden_grad = lax.dot_general(
            flat_grad,
            w_down[tower_index],
            (((1,), (1,)), ((), ())),
            preferred_element_type=jnp.float32,
        )
        gate_grad = gelu_back(hidden_grad * up_pre)[0].astype(jnp.bfloat16)
        up_grad = (hidden_grad * activated).astype(jnp.bfloat16)
        return (normed, gate_grad, up_grad, hidden, flat_grad)

    towers_back = (
        backward_part(query_parts, query_rows, 0),
        backward_part(passage_parts, passage_rows, 1),
    )

    def weight_terms():
        matrices = [[], [], []]
        for normed, gate_grad, up_grad, hidden, flat_grad in towers_back:
            matrices[0].append(contract(normed, gate_grad))
            matrices[1].append(contract(normed, up_grad))
            matrices[2].append(contract(flat_grad, hidden))
        return jnp.stack([jnp.stack(pieces, axis=1) for pieces in matrices], axis=1)

    summed_grads = lax.psum_scatter(weight_terms(), "dp", scatter_dimension=0, tiled=True)
    grad_gate = jnp.transpose(summed_grads[:, 0], (1, 0, 2))
    grad_up = jnp.transpose(summed_grads[:, 1], (1, 0, 2))
    grad_down = jnp.transpose(summed_grads[:, 2], (1, 2, 0))
    return (grad_gate, grad_up, grad_down)


def solution(mesh):
    return jax.shard_map(
        body,
        mesh=mesh,
        in_specs=(
            P("dp", None, None),
            P("dp", None, None),
            P("dp", None),
            P("dp", None),
            P(),
            P(),
            P(None, None, "segment"),
            P(None, None, "segment"),
            P(None, "segment", None),
            P(),
            P("dp"),
            P("dp", None),
            P("dp"),
        ),
        out_specs=(P(None, "dp", "segment"), P(None, "dp", "segment"), P(None, "segment", "dp")),
        check_vma=False,
    )
```

```python
import jax
import jax.numpy as jnp
from jax import lax
from jax.sharding import PartitionSpec as P

score_temp = 0.05
rank_temp = 1.0
recall_depth = 5.0
loss_scale = 16.0
norm_eps = 1e-06


def inverse_rms(values):
    return lax.rsqrt(jnp.mean(values * values, axis=-1, keepdims=True) + norm_eps)


def normed_input(states, ff_gain):
    widened = states.astype(jnp.float32)
    return (widened * inverse_rms(widened) * ff_gain).astype(jnp.bfloat16)


def pooled_embedding(summed, tokens, out_gain, proj_weight):
    normed = summed * inverse_rms(summed) * out_gain
    token_mask = (tokens != 0).astype(jnp.float32)[:, :, None]
    pooled = jnp.sum(normed * token_mask, axis=1) / jnp.sum(token_mask, axis=1)
    projected = jnp.dot(pooled, proj_weight.astype(jnp.float32), precision=lax.Precision.HIGHEST)
    return projected * lax.rsqrt(jnp.sum(projected * projected, axis=-1, keepdims=True) + norm_eps)


def recall_loss(scores, valid_mask):
    margins = (scores[:, 1:] - scores[:, :1]) / score_temp
    soft_ranks = 1.0 + jnp.sum(jax.nn.sigmoid(margins) * valid_mask, axis=1)
    return loss_scale * jnp.sum(jax.nn.sigmoid((soft_ranks - recall_depth - 0.5) / rank_temp))


def contract(left, right):
    return lax.dot_general(
        left, right, (((0,), (0,)), ((), ())), preferred_element_type=jnp.float32
    )


def natural_order(gathered, segments, groups, per_device):
    model_width = gathered.shape[-1]
    shaped = gathered.reshape(segments, groups, per_device, model_width)
    return jnp.transpose(shaped, (1, 0, 2, 3)).reshape(-1, model_width)


def score_grads_of(scores, counts):
    slots = scores.shape[1] - 1
    valid_mask = (
        lax.broadcasted_iota(jnp.int32, (scores.shape[0], slots), 1) < counts[:, None]
    ).astype(jnp.float32)
    return jax.grad(recall_loss)(scores, valid_mask)


def body(
    query_states,
    passage_states,
    query_tokens,
    passage_tokens,
    ff_gains,
    out_gains,
    w_gate,
    w_up,
    w_down,
    w_proj,
    positive_ids,
    negative_ids,
    negative_counts,
):
    segments = lax.axis_size("segment")
    groups = lax.axis_size("dp")
    segment_index = lax.axis_index("segment")
    model_width = query_states.shape[-1]
    query_dev = query_states.shape[0] // segments
    passage_dev = passage_states.shape[0] // segments

    def forward_part(states, tower_index):
        normed = normed_input(states, ff_gains[tower_index]).reshape(-1, model_width)
        gate_pre = jnp.dot(normed, w_gate[tower_index], preferred_element_type=jnp.float32)
        up_pre = jnp.dot(normed, w_up[tower_index], preferred_element_type=jnp.float32)
        activated, gelu_back = jax.vjp(jax.nn.gelu, gate_pre)
        hidden = (activated * up_pre).astype(jnp.bfloat16)
        branch = jnp.dot(hidden, w_down[tower_index], preferred_element_type=jnp.float32).reshape(
            states.shape
        )
        return (normed, up_pre, activated, gelu_back, hidden, branch)

    def own_rows(values, per_device):
        return lax.dynamic_slice_in_dim(values, segment_index * per_device, per_device, 0)

    def head_of(tokens, tower_index):
        return lambda summed: pooled_embedding(
            summed, tokens, out_gains[tower_index], w_proj[tower_index]
        )

    query_parts = forward_part(query_states, 0)
    passage_parts = forward_part(passage_states, 1)
    query_branch, passage_branch = (
        lax.psum_scatter(query_parts[5], "segment", scatter_dimension=0, tiled=True),
        lax.psum_scatter(passage_parts[5], "segment", scatter_dimension=0, tiled=True),
    )
    query_embed, query_back = jax.vjp(
        head_of(own_rows(query_tokens, query_dev), 0),
        own_rows(query_states, query_dev).astype(jnp.float32) + query_branch,
    )
    passage_embed, passage_back = jax.vjp(
        head_of(own_rows(passage_tokens, passage_dev), 1),
        own_rows(passage_states, passage_dev).astype(jnp.float32) + passage_branch,
    )
    query_round = query_embed.astype(jnp.bfloat16)
    passage_round = passage_embed.astype(jnp.bfloat16)
    id_radix = 256
    own_ids = jnp.concatenate(
        [own_rows(positive_ids, query_dev)[:, None], own_rows(negative_ids, query_dev)], axis=1
    )
    slots = own_ids.shape[1]
    own_meta = jnp.concatenate(
        [own_ids // id_radix, own_ids % id_radix, own_rows(negative_counts, query_dev)[:, None]],
        axis=1,
    ).astype(jnp.bfloat16)
    meta_width = own_meta.shape[1]
    meta_rows = -(-query_dev * meta_width // model_width)
    meta_flat = jnp.pad(
        own_meta.reshape(-1), (0, meta_rows * model_width - query_dev * meta_width)
    ).reshape(meta_rows, model_width)
    packed = jnp.concatenate([query_round, passage_round, meta_flat], axis=0)
    gathered = lax.all_gather(packed, ("dp", "segment"), axis=0, tiled=False)
    gathered = gathered.reshape(groups, segments, -1, model_width)
    query_all = gathered[:, :, :query_dev].reshape(-1, model_width)
    passage_all = gathered[:, :, query_dev : query_dev + passage_dev].reshape(-1, model_width)
    meta_all = (
        gathered[:, :, query_dev + passage_dev :]
        .reshape(groups, segments, -1)[:, :, : query_dev * meta_width]
        .reshape(-1, meta_width)
        .astype(jnp.int32)
    )
    cand_all = meta_all[:, :slots] * id_radix + meta_all[:, slots : 2 * slots]
    counts_all = meta_all[:, 2 * slots]
    passage_total = passage_all.shape[0]
    all_scores = lax.dot_general(
        query_all, passage_all, (((1,), (1,)), ((), ())), preferred_element_type=jnp.float32
    )
    scores = jnp.take_along_axis(all_scores, cand_all, axis=1)
    score_grads = score_grads_of(scores, counts_all)
    dp_index = lax.axis_index("dp")
    query_start = (dp_index * segments + segment_index) * query_dev
    passage_start = (dp_index * segments + segment_index) * passage_dev
    own_cand = lax.dynamic_slice_in_dim(cand_all, query_start, query_dev, 0)
    own_grads = lax.dynamic_slice_in_dim(score_grads, query_start, query_dev, 0)
    every_id = lax.broadcasted_iota(jnp.int32, (1, 1, passage_total), 2)
    query_coef = jnp.sum(
        jnp.where(own_cand[:, :, None] == every_id, own_grads[:, :, None], 0.0), axis=1
    )
    own_passages = passage_start + lax.broadcasted_iota(jnp.int32, (1, 1, passage_dev), 2)
    passage_coef = jnp.sum(
        jnp.where(cand_all[:, :, None] == own_passages, score_grads[:, :, None], 0.0), axis=1
    )
    query_grad = jnp.dot(
        query_coef, passage_all.astype(jnp.float32), precision=lax.Precision.HIGHEST
    )
    passage_grad = lax.dot_general(
        passage_coef,
        query_all.astype(jnp.float32),
        (((0,), (0,)), ((), ())),
        precision=lax.Precision.HIGHEST,
        preferred_element_type=jnp.float32,
    )
    query_share = query_back(query_grad)[0].astype(jnp.bfloat16)
    passage_share = passage_back(passage_grad)[0].astype(jnp.bfloat16)
    query_rows, passage_rows = (
        lax.all_gather(query_share, "segment", axis=0, tiled=True),
        lax.all_gather(passage_share, "segment", axis=0, tiled=True),
    )

    def backward_part(tower_parts, row_grads, tower_index):
        normed, up_pre, activated, gelu_back, hidden, branch = tower_parts
        flat_grad = row_grads.reshape(-1, model_width)
        hidden_grad = lax.dot_general(
            flat_grad,
            w_down[tower_index],
            (((1,), (1,)), ((), ())),
            preferred_element_type=jnp.float32,
        )
        gate_grad = gelu_back(hidden_grad * up_pre)[0].astype(jnp.bfloat16)
        up_grad = (hidden_grad * activated).astype(jnp.bfloat16)
        return (normed, gate_grad, up_grad, hidden, flat_grad)

    towers_back = (
        backward_part(query_parts, query_rows, 0),
        backward_part(passage_parts, passage_rows, 1),
    )

    def weight_terms():
        matrices = [[], [], []]
        for normed, gate_grad, up_grad, hidden, flat_grad in towers_back:
            matrices[0].append(contract(normed, gate_grad))
            matrices[1].append(contract(normed, up_grad))
            matrices[2].append(contract(flat_grad, hidden))
        return jnp.stack([jnp.stack(pieces, axis=1) for pieces in matrices], axis=1)

    summed_grads = lax.psum_scatter(weight_terms(), "dp", scatter_dimension=0, tiled=True)
    grad_gate = jnp.transpose(summed_grads[:, 0], (1, 0, 2))
    grad_up = jnp.transpose(summed_grads[:, 1], (1, 0, 2))
    grad_down = jnp.transpose(summed_grads[:, 2], (1, 2, 0))
    return (grad_gate, grad_up, grad_down)


def solution(mesh):
    return jax.shard_map(
        body,
        mesh=mesh,
        in_specs=(
            P("dp", None, None),
            P("dp", None, None),
            P("dp", None),
            P("dp", None),
            P(),
            P(),
            P(None, None, "segment"),
            P(None, None, "segment"),
            P(None, "segment", None),
            P(),
            P("dp"),
            P("dp", None),
            P("dp"),
        ),
        out_specs=(P(None, "dp", "segment"), P(None, "dp", "segment"), P(None, "segment", "dp")),
        check_vma=False,
    )
```

```python
import jax
import jax.numpy as jnp
from jax import lax
from jax.sharding import PartitionSpec as P

score_temp = 0.05
rank_temp = 1.0
recall_depth = 5.0
loss_scale = 16.0
norm_eps = 1e-06


def inverse_rms(values):
    return lax.rsqrt(jnp.mean(values * values, axis=-1, keepdims=True) + norm_eps)


def normed_input(states, ff_gain):
    widened = states.astype(jnp.float32)
    return (widened * inverse_rms(widened) * ff_gain).astype(jnp.bfloat16)


def pooled_embedding(summed, tokens, out_gain, proj_weight):
    normed = summed * inverse_rms(summed) * out_gain
    token_mask = (tokens != 0).astype(jnp.float32)[:, :, None]
    pooled = jnp.sum(normed * token_mask, axis=1) / jnp.sum(token_mask, axis=1)
    projected = jnp.dot(pooled, proj_weight.astype(jnp.float32), precision=lax.Precision.HIGHEST)
    return projected * lax.rsqrt(jnp.sum(projected * projected, axis=-1, keepdims=True) + norm_eps)


def recall_loss(scores, valid_mask):
    margins = (scores[:, 1:] - scores[:, :1]) / score_temp
    soft_ranks = 1.0 + jnp.sum(jax.nn.sigmoid(margins) * valid_mask, axis=1)
    return loss_scale * jnp.sum(jax.nn.sigmoid((soft_ranks - recall_depth - 0.5) / rank_temp))


def contract(left, right):
    return lax.dot_general(
        left, right, (((0,), (0,)), ((), ())), preferred_element_type=jnp.float32
    )


def natural_order(gathered, segments, groups, per_device):
    model_width = gathered.shape[-1]
    shaped = gathered.reshape(segments, groups, per_device, model_width)
    return jnp.transpose(shaped, (1, 0, 2, 3)).reshape(-1, model_width)


def score_grads_of(scores, counts):
    slots = scores.shape[1] - 1
    valid_mask = (
        lax.broadcasted_iota(jnp.int32, (scores.shape[0], slots), 1) < counts[:, None]
    ).astype(jnp.float32)
    return jax.grad(recall_loss)(scores, valid_mask)


def body(
    query_states,
    passage_states,
    query_tokens,
    passage_tokens,
    ff_gains,
    out_gains,
    w_gate,
    w_up,
    w_down,
    w_proj,
    positive_ids,
    negative_ids,
    negative_counts,
):
    segments = lax.axis_size("segment")
    groups = lax.axis_size("dp")
    segment_index = lax.axis_index("segment")
    model_width = query_states.shape[-1]
    query_dev = query_states.shape[0] // segments
    passage_dev = passage_states.shape[0] // segments

    def forward_part(states, tower_index):
        normed = normed_input(states, ff_gains[tower_index]).reshape(-1, model_width)
        gate_pre = jnp.dot(normed, w_gate[tower_index], preferred_element_type=jnp.float32)
        up_pre = jnp.dot(normed, w_up[tower_index], preferred_element_type=jnp.float32)
        activated, gelu_back = jax.vjp(jax.nn.gelu, gate_pre)
        hidden = (activated * up_pre).astype(jnp.bfloat16)
        branch = jnp.dot(hidden, w_down[tower_index], preferred_element_type=jnp.float32).reshape(
            states.shape
        )
        return (normed, up_pre, activated, gelu_back, hidden, branch)

    def own_rows(values, per_device):
        return lax.dynamic_slice_in_dim(values, segment_index * per_device, per_device, 0)

    def head_of(tokens, tower_index):
        return lambda summed: pooled_embedding(
            summed, tokens, out_gains[tower_index], w_proj[tower_index]
        )

    query_parts = forward_part(query_states, 0)
    passage_parts = forward_part(passage_states, 1)
    query_branch, passage_branch = (
        lax.psum_scatter(query_parts[5], "segment", scatter_dimension=0, tiled=True),
        lax.psum_scatter(passage_parts[5], "segment", scatter_dimension=0, tiled=True),
    )
    query_embed, query_back = jax.vjp(
        head_of(own_rows(query_tokens, query_dev), 0),
        own_rows(query_states, query_dev).astype(jnp.float32) + query_branch,
    )
    passage_embed, passage_back = jax.vjp(
        head_of(own_rows(passage_tokens, passage_dev), 1),
        own_rows(passage_states, passage_dev).astype(jnp.float32) + passage_branch,
    )
    query_round = query_embed.astype(jnp.bfloat16)
    passage_round = passage_embed.astype(jnp.bfloat16)
    id_radix = 256
    own_ids = jnp.concatenate(
        [own_rows(positive_ids, query_dev)[:, None], own_rows(negative_ids, query_dev)], axis=1
    )
    slots = own_ids.shape[1]
    own_meta = jnp.concatenate(
        [own_ids // id_radix, own_ids % id_radix, own_rows(negative_counts, query_dev)[:, None]],
        axis=1,
    ).astype(jnp.bfloat16)
    meta_width = own_meta.shape[1]
    meta_rows = -(-query_dev * meta_width // model_width)
    meta_flat = jnp.pad(
        own_meta.reshape(-1), (0, meta_rows * model_width - query_dev * meta_width)
    ).reshape(meta_rows, model_width)
    packed = jnp.concatenate([query_round, passage_round, meta_flat], axis=0)
    gathered = lax.all_gather(packed, ("dp", "segment"), axis=0, tiled=False)
    gathered = gathered.reshape(groups, segments, -1, model_width)
    query_all = gathered[:, :, :query_dev].reshape(-1, model_width)
    passage_all = gathered[:, :, query_dev : query_dev + passage_dev].reshape(-1, model_width)
    meta_all = (
        gathered[:, :, query_dev + passage_dev :]
        .reshape(groups, segments, -1)[:, :, : query_dev * meta_width]
        .reshape(-1, meta_width)
        .astype(jnp.int32)
    )
    cand_all = meta_all[:, :slots] * id_radix + meta_all[:, slots : 2 * slots]
    counts_all = meta_all[:, 2 * slots]
    passage_total = passage_all.shape[0]
    all_scores = lax.dot_general(
        query_all, passage_all, (((1,), (1,)), ((), ())), preferred_element_type=jnp.float32
    )
    every_id = lax.broadcasted_iota(jnp.int32, (1, 1, passage_total), 2)
    scores = jnp.sum(
        jnp.where(cand_all[:, :, None] == every_id, all_scores[:, None, :], 0.0), axis=2
    )
    score_grads = score_grads_of(scores, counts_all)
    dp_index = lax.axis_index("dp")
    query_start = (dp_index * segments + segment_index) * query_dev
    passage_start = (dp_index * segments + segment_index) * passage_dev
    own_cand = lax.dynamic_slice_in_dim(cand_all, query_start, query_dev, 0)
    own_grads = lax.dynamic_slice_in_dim(score_grads, query_start, query_dev, 0)
    query_coef = jnp.sum(
        jnp.where(own_cand[:, :, None] == every_id, own_grads[:, :, None], 0.0), axis=1
    )
    own_passages = passage_start + lax.broadcasted_iota(jnp.int32, (1, 1, passage_dev), 2)
    passage_coef = jnp.sum(
        jnp.where(cand_all[:, :, None] == own_passages, score_grads[:, :, None], 0.0), axis=1
    )
    query_grad = jnp.dot(
        query_coef, passage_all.astype(jnp.float32), precision=lax.Precision.HIGHEST
    )
    passage_grad = lax.dot_general(
        passage_coef,
        query_all.astype(jnp.float32),
        (((0,), (0,)), ((), ())),
        precision=lax.Precision.HIGHEST,
        preferred_element_type=jnp.float32,
    )
    query_share = query_back(query_grad)[0].astype(jnp.bfloat16)
    passage_share = passage_back(passage_grad)[0].astype(jnp.bfloat16)
    query_rows, passage_rows = (
        lax.all_gather(query_share, "segment", axis=0, tiled=True),
        lax.all_gather(passage_share, "segment", axis=0, tiled=True),
    )

    def backward_part(tower_parts, row_grads, tower_index):
        normed, up_pre, activated, gelu_back, hidden, branch = tower_parts
        flat_grad = row_grads.reshape(-1, model_width)
        hidden_grad = lax.dot_general(
            flat_grad,
            w_down[tower_index],
            (((1,), (1,)), ((), ())),
            preferred_element_type=jnp.float32,
        )
        gate_grad = gelu_back(hidden_grad * up_pre)[0].astype(jnp.bfloat16)
        up_grad = (hidden_grad * activated).astype(jnp.bfloat16)
        return (normed, gate_grad, up_grad, hidden, flat_grad)

    towers_back = (
        backward_part(query_parts, query_rows, 0),
        backward_part(passage_parts, passage_rows, 1),
    )

    def weight_terms():
        matrices = [[], [], []]
        for normed, gate_grad, up_grad, hidden, flat_grad in towers_back:
            matrices[0].append(contract(normed, gate_grad))
            matrices[1].append(contract(normed, up_grad))
            matrices[2].append(contract(flat_grad, hidden))
        return jnp.stack([jnp.stack(pieces, axis=1) for pieces in matrices], axis=1)

    summed_grads = lax.psum_scatter(weight_terms(), "dp", scatter_dimension=0, tiled=True)
    grad_gate = jnp.transpose(summed_grads[:, 0], (1, 0, 2))
    grad_up = jnp.transpose(summed_grads[:, 1], (1, 0, 2))
    grad_down = jnp.transpose(summed_grads[:, 2], (1, 2, 0))
    return (grad_gate, grad_up, grad_down)


def solution(mesh):
    return jax.shard_map(
        body,
        mesh=mesh,
        in_specs=(
            P("dp", None, None),
            P("dp", None, None),
            P("dp", None),
            P("dp", None),
            P(),
            P(),
            P(None, None, "segment"),
            P(None, None, "segment"),
            P(None, "segment", None),
            P(),
            P("dp"),
            P("dp", None),
            P("dp"),
        ),
        out_specs=(P(None, "dp", "segment"), P(None, "dp", "segment"), P(None, "segment", "dp")),
        check_vma=False,
    )
```

```python
import jax
import jax.numpy as jnp
from jax import lax
from jax.sharding import PartitionSpec as P

score_temp = 0.05
rank_temp = 1.0
recall_depth = 5.0
loss_scale = 16.0
norm_eps = 1e-06


def inverse_rms(values):
    return lax.rsqrt(jnp.mean(values * values, axis=-1, keepdims=True) + norm_eps)


def normed_input(states, ff_gain):
    widened = states.astype(jnp.float32)
    return (widened * inverse_rms(widened) * ff_gain).astype(jnp.bfloat16)


def pooled_embedding(summed, tokens, out_gain, proj_weight):
    normed = summed * inverse_rms(summed) * out_gain
    token_mask = (tokens != 0).astype(jnp.float32)[:, :, None]
    pooled = jnp.sum(normed * token_mask, axis=1) / jnp.sum(token_mask, axis=1)
    projected = jnp.dot(pooled, proj_weight.astype(jnp.float32), precision=lax.Precision.HIGHEST)
    return projected * lax.rsqrt(jnp.sum(projected * projected, axis=-1, keepdims=True) + norm_eps)


def recall_loss(scores, valid_mask):
    margins = (scores[:, 1:] - scores[:, :1]) / score_temp
    soft_ranks = 1.0 + jnp.sum(jax.nn.sigmoid(margins) * valid_mask, axis=1)
    return loss_scale * jnp.sum(jax.nn.sigmoid((soft_ranks - recall_depth - 0.5) / rank_temp))


def contract(left, right):
    return lax.dot_general(
        left, right, (((0,), (0,)), ((), ())), preferred_element_type=jnp.float32
    )


def natural_order(gathered, segments, groups, per_device):
    model_width = gathered.shape[-1]
    shaped = gathered.reshape(segments, groups, per_device, model_width)
    return jnp.transpose(shaped, (1, 0, 2, 3)).reshape(-1, model_width)


def score_grads_of(scores, counts):
    slots = scores.shape[1] - 1
    valid_mask = (
        lax.broadcasted_iota(jnp.int32, (scores.shape[0], slots), 1) < counts[:, None]
    ).astype(jnp.float32)
    return jax.grad(recall_loss)(scores, valid_mask)


def body(
    query_states,
    passage_states,
    query_tokens,
    passage_tokens,
    ff_gains,
    out_gains,
    w_gate,
    w_up,
    w_down,
    w_proj,
    positive_ids,
    negative_ids,
    negative_counts,
):
    segments = lax.axis_size("segment")
    groups = lax.axis_size("dp")
    segment_index = lax.axis_index("segment")
    model_width = query_states.shape[-1]
    query_dev = query_states.shape[0] // segments
    passage_dev = passage_states.shape[0] // segments

    def forward_part(states, tower_index):
        normed = normed_input(states, ff_gains[tower_index]).reshape(-1, model_width)
        gate_pre = jnp.dot(normed, w_gate[tower_index], preferred_element_type=jnp.float32)
        up_pre = jnp.dot(normed, w_up[tower_index], preferred_element_type=jnp.float32)
        activated, gelu_back = jax.vjp(jax.nn.gelu, gate_pre)
        hidden = (activated * up_pre).astype(jnp.bfloat16)
        branch = jnp.dot(hidden, w_down[tower_index], preferred_element_type=jnp.float32).reshape(
            states.shape
        )
        return (normed, up_pre, activated, gelu_back, hidden, branch)

    def own_rows(values, per_device):
        return lax.dynamic_slice_in_dim(values, segment_index * per_device, per_device, 0)

    def head_of(tokens, tower_index):
        return lambda summed: pooled_embedding(
            summed, tokens, out_gains[tower_index], w_proj[tower_index]
        )

    query_parts = forward_part(query_states, 0)
    passage_parts = forward_part(passage_states, 1)
    query_branch, passage_branch = (
        lax.psum_scatter(query_parts[5], "segment", scatter_dimension=0, tiled=True),
        lax.psum_scatter(passage_parts[5], "segment", scatter_dimension=0, tiled=True),
    )
    query_embed, query_back = jax.vjp(
        head_of(own_rows(query_tokens, query_dev), 0),
        own_rows(query_states, query_dev).astype(jnp.float32) + query_branch,
    )
    passage_embed, passage_back = jax.vjp(
        head_of(own_rows(passage_tokens, passage_dev), 1),
        own_rows(passage_states, passage_dev).astype(jnp.float32) + passage_branch,
    )
    query_round = query_embed.astype(jnp.bfloat16)
    passage_round = passage_embed.astype(jnp.bfloat16)
    id_radix = 256
    own_ids = jnp.concatenate(
        [own_rows(positive_ids, query_dev)[:, None], own_rows(negative_ids, query_dev)], axis=1
    )
    slots = own_ids.shape[1]
    own_meta = jnp.concatenate(
        [own_ids // id_radix, own_ids % id_radix, own_rows(negative_counts, query_dev)[:, None]],
        axis=1,
    ).astype(jnp.bfloat16)
    meta_width = own_meta.shape[1]
    meta_rows = -(-query_dev * meta_width // model_width)
    meta_flat = jnp.pad(
        own_meta.reshape(-1), (0, meta_rows * model_width - query_dev * meta_width)
    ).reshape(meta_rows, model_width)
    packed = jnp.concatenate([query_round, passage_round, meta_flat], axis=0)
    gathered = lax.all_gather(packed, ("dp", "segment"), axis=0, tiled=False)
    gathered = gathered.reshape(groups, segments, -1, model_width)
    query_all = gathered[:, :, :query_dev].reshape(-1, model_width)
    passage_all = gathered[:, :, query_dev : query_dev + passage_dev].reshape(-1, model_width)
    meta_all = (
        gathered[:, :, query_dev + passage_dev :]
        .reshape(groups, segments, -1)[:, :, : query_dev * meta_width]
        .reshape(-1, meta_width)
        .astype(jnp.int32)
    )
    cand_all = meta_all[:, :slots] * id_radix + meta_all[:, slots : 2 * slots]
    counts_all = meta_all[:, 2 * slots]
    passage_total = passage_all.shape[0]
    all_scores = lax.dot_general(
        query_all, passage_all, (((1,), (1,)), ((), ())), preferred_element_type=jnp.float32
    )
    every_id = lax.broadcasted_iota(jnp.int32, (1, 1, passage_total), 2)
    scores = jnp.sum(
        jnp.where(cand_all[:, :, None] == every_id, all_scores[:, None, :], 0.0), axis=2
    )
    score_grads = score_grads_of(scores, counts_all)
    dp_index = lax.axis_index("dp")
    query_start = (dp_index * segments + segment_index) * query_dev
    passage_start = (dp_index * segments + segment_index) * passage_dev
    own_cand = lax.dynamic_slice_in_dim(cand_all, query_start, query_dev, 0)
    own_grads = lax.dynamic_slice_in_dim(score_grads, query_start, query_dev, 0)
    query_coef = jnp.sum(
        jnp.where(own_cand[:, :, None] == every_id, own_grads[:, :, None], 0.0), axis=1
    )
    own_passages = passage_start + lax.broadcasted_iota(jnp.int32, (1, 1, passage_dev), 2)
    passage_coef = jnp.sum(
        jnp.where(cand_all[:, :, None] == own_passages, score_grads[:, :, None], 0.0), axis=1
    )
    query_grad = jnp.dot(
        query_coef, passage_all.astype(jnp.float32), precision=lax.Precision.HIGHEST
    )
    passage_grad = lax.dot_general(
        passage_coef,
        query_all.astype(jnp.float32),
        (((0,), (0,)), ((), ())),
        precision=lax.Precision.HIGHEST,
        preferred_element_type=jnp.float32,
    )
    query_share = query_back(query_grad)[0].astype(jnp.bfloat16)
    passage_share = passage_back(passage_grad)[0].astype(jnp.bfloat16)
    query_rows, passage_rows = (
        lax.all_gather(query_share, "segment", axis=0, tiled=True),
        lax.all_gather(passage_share, "segment", axis=0, tiled=True),
    )

    def backward_part(tower_parts, row_grads, tower_index):
        normed, up_pre, activated, gelu_back, hidden, branch = tower_parts
        flat_grad = row_grads.reshape(-1, model_width)
        hidden_grad = lax.dot_general(
            flat_grad,
            w_down[tower_index],
            (((1,), (1,)), ((), ())),
            preferred_element_type=jnp.float32,
        )
        gate_grad = gelu_back(hidden_grad * up_pre)[0].astype(jnp.bfloat16)
        up_grad = (hidden_grad * activated).astype(jnp.bfloat16)
        return (normed, gate_grad, up_grad, hidden, flat_grad)

    towers_back = (
        backward_part(query_parts, query_rows, 0),
        backward_part(passage_parts, passage_rows, 1),
    )

    def weight_terms():
        matrices = [[], [], []]
        for normed, gate_grad, up_grad, hidden, flat_grad in towers_back:
            matrices[0].append(contract(normed, gate_grad))
            matrices[1].append(contract(normed, up_grad))
            matrices[2].append(contract(flat_grad, hidden))
        return jnp.stack([jnp.stack(pieces, axis=1) for pieces in matrices], axis=1)

    summed_grads = lax.psum_scatter(
        weight_terms().astype(jnp.bfloat16), "dp", scatter_dimension=0, tiled=True
    ).astype(jnp.float32)
    grad_gate = jnp.transpose(summed_grads[:, 0], (1, 0, 2))
    grad_up = jnp.transpose(summed_grads[:, 1], (1, 0, 2))
    grad_down = jnp.transpose(summed_grads[:, 2], (1, 2, 0))
    return (grad_gate, grad_up, grad_down)


def solution(mesh):
    return jax.shard_map(
        body,
        mesh=mesh,
        in_specs=(
            P("dp", None, None),
            P("dp", None, None),
            P("dp", None),
            P("dp", None),
            P(),
            P(),
            P(None, None, "segment"),
            P(None, None, "segment"),
            P(None, "segment", None),
            P(),
            P("dp"),
            P("dp", None),
            P("dp"),
        ),
        out_specs=(P(None, "dp", "segment"), P(None, "dp", "segment"), P(None, "segment", "dp")),
        check_vma=False,
    )
```

```python
import jax
import jax.numpy as jnp
from jax import lax
from jax.sharding import PartitionSpec as P

score_temp = 0.05
rank_temp = 1.0
recall_depth = 5.0
loss_scale = 16.0
norm_eps = 1e-06


def inverse_rms(values):
    return lax.rsqrt(jnp.mean(values * values, axis=-1, keepdims=True) + norm_eps)


def normed_input(states, ff_gain):
    widened = states.astype(jnp.float32)
    return (widened * inverse_rms(widened) * ff_gain).astype(jnp.bfloat16)


def pooled_embedding(summed, tokens, out_gain, proj_weight):
    normed = summed * inverse_rms(summed) * out_gain
    token_mask = (tokens != 0).astype(jnp.float32)[:, :, None]
    pooled = jnp.sum(normed * token_mask, axis=1) / jnp.sum(token_mask, axis=1)
    projected = jnp.dot(pooled, proj_weight.astype(jnp.float32), precision=lax.Precision.HIGHEST)
    return projected * lax.rsqrt(jnp.sum(projected * projected, axis=-1, keepdims=True) + norm_eps)


def recall_loss(scores, valid_mask):
    margins = (scores[:, 1:] - scores[:, :1]) / score_temp
    soft_ranks = 1.0 + jnp.sum(jax.nn.sigmoid(margins) * valid_mask, axis=1)
    return loss_scale * jnp.sum(jax.nn.sigmoid((soft_ranks - recall_depth - 0.5) / rank_temp))


def contract(left, right):
    return lax.dot_general(
        left, right, (((0,), (0,)), ((), ())), preferred_element_type=jnp.float32
    )


def natural_order(gathered, segments, groups, per_device):
    model_width = gathered.shape[-1]
    shaped = gathered.reshape(segments, groups, per_device, model_width)
    return jnp.transpose(shaped, (1, 0, 2, 3)).reshape(-1, model_width)


def score_grads_of(scores, counts):
    slots = scores.shape[1] - 1
    valid_mask = (
        lax.broadcasted_iota(jnp.int32, (scores.shape[0], slots), 1) < counts[:, None]
    ).astype(jnp.float32)
    return jax.grad(recall_loss)(scores, valid_mask)


def body(
    query_states,
    passage_states,
    query_tokens,
    passage_tokens,
    ff_gains,
    out_gains,
    w_gate,
    w_up,
    w_down,
    w_proj,
    positive_ids,
    negative_ids,
    negative_counts,
):
    segments = lax.axis_size("segment")
    groups = lax.axis_size("dp")
    segment_index = lax.axis_index("segment")
    model_width = query_states.shape[-1]
    query_dev = query_states.shape[0] // segments
    passage_dev = passage_states.shape[0] // segments

    def forward_part(states, tower_index):
        normed = normed_input(states, ff_gains[tower_index]).reshape(-1, model_width)
        gate_pre = jnp.dot(normed, w_gate[tower_index], preferred_element_type=jnp.float32)
        up_pre = jnp.dot(normed, w_up[tower_index], preferred_element_type=jnp.float32)
        activated, gelu_back = jax.vjp(jax.nn.gelu, gate_pre)
        hidden = (activated * up_pre).astype(jnp.bfloat16)
        branch = jnp.dot(hidden, w_down[tower_index], preferred_element_type=jnp.float32).reshape(
            states.shape
        )
        return (normed, up_pre, activated, gelu_back, hidden, branch)

    def own_rows(values, per_device):
        return lax.dynamic_slice_in_dim(values, segment_index * per_device, per_device, 0)

    def head_of(tokens, tower_index):
        return lambda summed: pooled_embedding(
            summed, tokens, out_gains[tower_index], w_proj[tower_index]
        )

    query_parts = forward_part(query_states, 0)
    passage_parts = forward_part(passage_states, 1)
    query_block = query_parts[5].reshape(segments, -1, model_width)
    passage_block = passage_parts[5].reshape(segments, -1, model_width)
    query_size = query_block.shape[1]
    branch_sum = lax.psum_scatter(
        jnp.concatenate([query_block, passage_block], axis=1),
        "segment",
        scatter_dimension=0,
        tiled=True,
    )[0]
    query_branch = branch_sum[:query_size].reshape((query_dev,) + query_states.shape[1:])
    passage_branch = branch_sum[query_size:].reshape((passage_dev,) + passage_states.shape[1:])
    query_embed, query_back = jax.vjp(
        head_of(own_rows(query_tokens, query_dev), 0),
        own_rows(query_states, query_dev).astype(jnp.float32) + query_branch,
    )
    passage_embed, passage_back = jax.vjp(
        head_of(own_rows(passage_tokens, passage_dev), 1),
        own_rows(passage_states, passage_dev).astype(jnp.float32) + passage_branch,
    )
    query_round = query_embed.astype(jnp.bfloat16)
    passage_round = passage_embed.astype(jnp.bfloat16)
    id_radix = 256
    own_ids = jnp.concatenate(
        [own_rows(positive_ids, query_dev)[:, None], own_rows(negative_ids, query_dev)], axis=1
    )
    slots = own_ids.shape[1]
    own_meta = jnp.concatenate(
        [own_ids // id_radix, own_ids % id_radix, own_rows(negative_counts, query_dev)[:, None]],
        axis=1,
    ).astype(jnp.bfloat16)
    meta_width = own_meta.shape[1]
    meta_rows = -(-query_dev * meta_width // model_width)
    meta_flat = jnp.pad(
        own_meta.reshape(-1), (0, meta_rows * model_width - query_dev * meta_width)
    ).reshape(meta_rows, model_width)
    packed = jnp.concatenate([query_round, passage_round, meta_flat], axis=0)
    gathered = lax.all_gather(packed, ("dp", "segment"), axis=0, tiled=False)
    gathered = gathered.reshape(groups, segments, -1, model_width)
    query_all = gathered[:, :, :query_dev].reshape(-1, model_width)
    passage_all = gathered[:, :, query_dev : query_dev + passage_dev].reshape(-1, model_width)
    meta_all = (
        gathered[:, :, query_dev + passage_dev :]
        .reshape(groups, segments, -1)[:, :, : query_dev * meta_width]
        .reshape(-1, meta_width)
        .astype(jnp.int32)
    )
    cand_all = meta_all[:, :slots] * id_radix + meta_all[:, slots : 2 * slots]
    counts_all = meta_all[:, 2 * slots]
    passage_total = passage_all.shape[0]
    all_scores = lax.dot_general(
        query_all, passage_all, (((1,), (1,)), ((), ())), preferred_element_type=jnp.float32
    )
    every_id = lax.broadcasted_iota(jnp.int32, (1, 1, passage_total), 2)
    scores = jnp.sum(
        jnp.where(cand_all[:, :, None] == every_id, all_scores[:, None, :], 0.0), axis=2
    )
    score_grads = score_grads_of(scores, counts_all)
    dp_index = lax.axis_index("dp")
    query_start = (dp_index * segments + segment_index) * query_dev
    passage_start = (dp_index * segments + segment_index) * passage_dev
    own_cand = lax.dynamic_slice_in_dim(cand_all, query_start, query_dev, 0)
    own_grads = lax.dynamic_slice_in_dim(score_grads, query_start, query_dev, 0)
    query_coef = jnp.sum(
        jnp.where(own_cand[:, :, None] == every_id, own_grads[:, :, None], 0.0), axis=1
    )
    own_passages = passage_start + lax.broadcasted_iota(jnp.int32, (1, 1, passage_dev), 2)
    passage_coef = jnp.sum(
        jnp.where(cand_all[:, :, None] == own_passages, score_grads[:, :, None], 0.0), axis=1
    )
    query_grad = jnp.dot(
        query_coef, passage_all.astype(jnp.float32), precision=lax.Precision.HIGHEST
    )
    passage_grad = lax.dot_general(
        passage_coef,
        query_all.astype(jnp.float32),
        (((0,), (0,)), ((), ())),
        precision=lax.Precision.HIGHEST,
        preferred_element_type=jnp.float32,
    )
    query_share = query_back(query_grad)[0].astype(jnp.bfloat16)
    passage_share = passage_back(passage_grad)[0].astype(jnp.bfloat16)
    share_rows = lax.all_gather(
        jnp.concatenate(
            [query_share.reshape(-1, model_width), passage_share.reshape(-1, model_width)], axis=0
        ),
        "segment",
        axis=0,
        tiled=False,
    )
    query_rows = share_rows[:, :query_size].reshape(query_states.shape)
    passage_rows = share_rows[:, query_size:].reshape(passage_states.shape)

    def backward_part(tower_parts, row_grads, tower_index):
        normed, up_pre, activated, gelu_back, hidden, branch = tower_parts
        flat_grad = row_grads.reshape(-1, model_width)
        hidden_grad = lax.dot_general(
            flat_grad,
            w_down[tower_index],
            (((1,), (1,)), ((), ())),
            preferred_element_type=jnp.float32,
        )
        gate_grad = gelu_back(hidden_grad * up_pre)[0].astype(jnp.bfloat16)
        up_grad = (hidden_grad * activated).astype(jnp.bfloat16)
        return (normed, gate_grad, up_grad, hidden, flat_grad)

    towers_back = (
        backward_part(query_parts, query_rows, 0),
        backward_part(passage_parts, passage_rows, 1),
    )

    def weight_terms():
        matrices = [[], [], []]
        for normed, gate_grad, up_grad, hidden, flat_grad in towers_back:
            matrices[0].append(contract(normed, gate_grad))
            matrices[1].append(contract(normed, up_grad))
            matrices[2].append(contract(flat_grad, hidden))
        return jnp.stack([jnp.stack(pieces, axis=1) for pieces in matrices], axis=1)

    summed_grads = lax.psum_scatter(weight_terms(), "dp", scatter_dimension=0, tiled=True)
    grad_gate = jnp.transpose(summed_grads[:, 0], (1, 0, 2))
    grad_up = jnp.transpose(summed_grads[:, 1], (1, 0, 2))
    grad_down = jnp.transpose(summed_grads[:, 2], (1, 2, 0))
    return (grad_gate, grad_up, grad_down)


def solution(mesh):
    return jax.shard_map(
        body,
        mesh=mesh,
        in_specs=(
            P("dp", None, None),
            P("dp", None, None),
            P("dp", None),
            P("dp", None),
            P(),
            P(),
            P(None, None, "segment"),
            P(None, None, "segment"),
            P(None, "segment", None),
            P(),
            P("dp"),
            P("dp", None),
            P("dp"),
        ),
        out_specs=(P(None, "dp", "segment"), P(None, "dp", "segment"), P(None, "segment", "dp")),
        check_vma=False,
    )
```

```python
import jax
import jax.numpy as jnp
from jax import lax
from jax.sharding import PartitionSpec as P

score_temp = 0.05
rank_temp = 1.0
recall_depth = 5.0
loss_scale = 16.0
norm_eps = 1e-06


def inverse_rms(values):
    return lax.rsqrt(jnp.mean(values * values, axis=-1, keepdims=True) + norm_eps)


def normed_input(states, ff_gain):
    widened = states.astype(jnp.float32)
    return (widened * inverse_rms(widened) * ff_gain).astype(jnp.bfloat16)


def pooled_embedding(summed, tokens, out_gain, proj_weight):
    normed = summed * inverse_rms(summed) * out_gain
    token_mask = (tokens != 0).astype(jnp.float32)[:, :, None]
    pooled = jnp.sum(normed * token_mask, axis=1) / jnp.sum(token_mask, axis=1)
    projected = jnp.dot(pooled, proj_weight.astype(jnp.float32), precision=lax.Precision.HIGHEST)
    return projected * lax.rsqrt(jnp.sum(projected * projected, axis=-1, keepdims=True) + norm_eps)


def recall_loss(scores, valid_mask):
    margins = (scores[:, 1:] - scores[:, :1]) / score_temp
    soft_ranks = 1.0 + jnp.sum(jax.nn.sigmoid(margins) * valid_mask, axis=1)
    return loss_scale * jnp.sum(jax.nn.sigmoid((soft_ranks - recall_depth - 0.5) / rank_temp))


def contract(left, right):
    return lax.dot_general(
        left, right, (((0,), (0,)), ((), ())), preferred_element_type=jnp.float32
    )


def natural_order(gathered, segments, groups, per_device):
    model_width = gathered.shape[-1]
    shaped = gathered.reshape(segments, groups, per_device, model_width)
    return jnp.transpose(shaped, (1, 0, 2, 3)).reshape(-1, model_width)


def score_grads_of(scores, counts):
    slots = scores.shape[1] - 1
    valid_mask = (
        lax.broadcasted_iota(jnp.int32, (scores.shape[0], slots), 1) < counts[:, None]
    ).astype(jnp.float32)
    return jax.grad(recall_loss)(scores, valid_mask)


def body(
    query_states,
    passage_states,
    query_tokens,
    passage_tokens,
    ff_gains,
    out_gains,
    w_gate,
    w_up,
    w_down,
    w_proj,
    positive_ids,
    negative_ids,
    negative_counts,
):
    segments = lax.axis_size("segment")
    groups = lax.axis_size("dp")
    segment_index = lax.axis_index("segment")
    model_width = query_states.shape[-1]
    query_dev = query_states.shape[0] // segments
    passage_dev = passage_states.shape[0] // segments

    def forward_part(states, tower_index):
        normed = normed_input(states, ff_gains[tower_index]).reshape(-1, model_width)
        gate_pre = jnp.dot(normed, w_gate[tower_index], preferred_element_type=jnp.float32)
        up_pre = jnp.dot(normed, w_up[tower_index], preferred_element_type=jnp.float32)
        activated, gelu_back = jax.vjp(jax.nn.gelu, gate_pre)
        hidden = (activated * up_pre).astype(jnp.bfloat16)
        branch = jnp.dot(hidden, w_down[tower_index], preferred_element_type=jnp.float32).reshape(
            states.shape
        )
        return (normed, up_pre, activated, gelu_back, hidden, branch)

    def own_rows(values, per_device):
        return lax.dynamic_slice_in_dim(values, segment_index * per_device, per_device, 0)

    def head_of(tokens, tower_index):
        return lambda summed: pooled_embedding(
            summed, tokens, out_gains[tower_index], w_proj[tower_index]
        )

    query_parts = forward_part(query_states, 0)
    passage_parts = forward_part(passage_states, 1)
    query_block = query_parts[5].reshape(segments, -1, model_width)
    passage_block = passage_parts[5].reshape(segments, -1, model_width)
    query_size = query_block.shape[1]
    branch_sum = lax.psum_scatter(
        jnp.concatenate([query_block, passage_block], axis=1),
        "segment",
        scatter_dimension=0,
        tiled=True,
    )[0]
    query_branch = branch_sum[:query_size].reshape((query_dev,) + query_states.shape[1:])
    passage_branch = branch_sum[query_size:].reshape((passage_dev,) + passage_states.shape[1:])
    query_embed, query_back = jax.vjp(
        head_of(own_rows(query_tokens, query_dev), 0),
        own_rows(query_states, query_dev).astype(jnp.float32) + query_branch,
    )
    passage_embed, passage_back = jax.vjp(
        head_of(own_rows(passage_tokens, passage_dev), 1),
        own_rows(passage_states, passage_dev).astype(jnp.float32) + passage_branch,
    )
    query_round = query_embed.astype(jnp.bfloat16)
    passage_round = passage_embed.astype(jnp.bfloat16)
    id_radix = 256
    own_ids = jnp.concatenate(
        [own_rows(positive_ids, query_dev)[:, None], own_rows(negative_ids, query_dev)], axis=1
    )
    slots = own_ids.shape[1]
    own_meta = jnp.concatenate(
        [own_ids // id_radix, own_ids % id_radix, own_rows(negative_counts, query_dev)[:, None]],
        axis=1,
    ).astype(jnp.bfloat16)
    meta_width = own_meta.shape[1]
    meta_rows = -(-query_dev * meta_width // model_width)
    meta_flat = jnp.pad(
        own_meta.reshape(-1), (0, meta_rows * model_width - query_dev * meta_width)
    ).reshape(meta_rows, model_width)
    packed = jnp.concatenate([query_round, passage_round, meta_flat], axis=0)
    devices = groups * segments
    gathered = lax.all_gather(packed[:, None, :], ("dp", "segment"), axis=1, tiled=True)
    query_all = gathered[:query_dev].reshape(-1, model_width)
    passage_all = gathered[query_dev : query_dev + passage_dev].reshape(-1, model_width)
    meta_all = (
        gathered[query_dev + passage_dev :]
        .transpose(1, 0, 2)
        .reshape(devices, -1)[:, : query_dev * meta_width]
        .reshape(devices, query_dev, meta_width)
        .transpose(1, 0, 2)
        .reshape(-1, meta_width)
        .astype(jnp.int32)
    )
    cand_ids = meta_all[:, :slots] * id_radix + meta_all[:, slots : 2 * slots]
    cand_all = (cand_ids % passage_dev) * devices + cand_ids // passage_dev
    counts_all = meta_all[:, 2 * slots]
    passage_total = passage_all.shape[0]
    all_scores = lax.dot_general(
        query_all, passage_all, (((1,), (1,)), ((), ())), preferred_element_type=jnp.float32
    )
    every_id = lax.broadcasted_iota(jnp.int32, (1, 1, passage_total), 2)
    scores = jnp.sum(
        jnp.where(cand_all[:, :, None] == every_id, all_scores[:, None, :], 0.0), axis=2
    )
    score_grads = score_grads_of(scores, counts_all)
    device_index = lax.axis_index("dp") * segments + segment_index
    own_cand = lax.dynamic_index_in_dim(
        cand_all.reshape(query_dev, devices, slots), device_index, 1, keepdims=False
    )
    own_grads = lax.dynamic_index_in_dim(
        score_grads.reshape(query_dev, devices, slots), device_index, 1, keepdims=False
    )
    query_coef = jnp.sum(
        jnp.where(own_cand[:, :, None] == every_id, own_grads[:, :, None], 0.0), axis=1
    )
    own_passages = (
        lax.broadcasted_iota(jnp.int32, (1, 1, passage_dev), 2) * devices + device_index
    )
    passage_coef = jnp.sum(
        jnp.where(cand_all[:, :, None] == own_passages, score_grads[:, :, None], 0.0), axis=1
    )
    query_grad = jnp.dot(
        query_coef, passage_all.astype(jnp.float32), precision=lax.Precision.HIGHEST
    )
    passage_grad = lax.dot_general(
        passage_coef,
        query_all.astype(jnp.float32),
        (((0,), (0,)), ((), ())),
        precision=lax.Precision.HIGHEST,
        preferred_element_type=jnp.float32,
    )
    query_share = query_back(query_grad)[0].astype(jnp.bfloat16)
    passage_share = passage_back(passage_grad)[0].astype(jnp.bfloat16)
    share_rows = lax.all_gather(
        jnp.concatenate(
            [query_share.reshape(-1, model_width), passage_share.reshape(-1, model_width)], axis=0
        ),
        "segment",
        axis=0,
        tiled=False,
    )
    query_rows = share_rows[:, :query_size].reshape(query_states.shape)
    passage_rows = share_rows[:, query_size:].reshape(passage_states.shape)

    def backward_part(tower_parts, row_grads, tower_index):
        normed, up_pre, activated, gelu_back, hidden, branch = tower_parts
        flat_grad = row_grads.reshape(-1, model_width)
        hidden_grad = lax.dot_general(
            flat_grad,
            w_down[tower_index],
            (((1,), (1,)), ((), ())),
            preferred_element_type=jnp.float32,
        )
        gate_grad = gelu_back(hidden_grad * up_pre)[0].astype(jnp.bfloat16)
        up_grad = (hidden_grad * activated).astype(jnp.bfloat16)
        return (normed, gate_grad, up_grad, hidden, flat_grad)

    towers_back = (
        backward_part(query_parts, query_rows, 0),
        backward_part(passage_parts, passage_rows, 1),
    )

    def weight_terms():
        matrices = [[], [], []]
        for normed, gate_grad, up_grad, hidden, flat_grad in towers_back:
            matrices[0].append(contract(normed, gate_grad))
            matrices[1].append(contract(normed, up_grad))
            matrices[2].append(contract(flat_grad, hidden))
        return jnp.stack([jnp.stack(pieces, axis=1) for pieces in matrices], axis=1)

    summed_grads = lax.psum_scatter(weight_terms(), "dp", scatter_dimension=0, tiled=True)
    grad_gate = jnp.transpose(summed_grads[:, 0], (1, 0, 2))
    grad_up = jnp.transpose(summed_grads[:, 1], (1, 0, 2))
    grad_down = jnp.transpose(summed_grads[:, 2], (1, 2, 0))
    return (grad_gate, grad_up, grad_down)


def solution(mesh):
    return jax.shard_map(
        body,
        mesh=mesh,
        in_specs=(
            P("dp", None, None),
            P("dp", None, None),
            P("dp", None),
            P("dp", None),
            P(),
            P(),
            P(None, None, "segment"),
            P(None, None, "segment"),
            P(None, "segment", None),
            P(),
            P("dp"),
            P("dp", None),
            P("dp"),
        ),
        out_specs=(P(None, "dp", "segment"), P(None, "dp", "segment"), P(None, "segment", "dp")),
        check_vma=False,
    )
```

```python
import jax
import jax.numpy as jnp
from jax import lax
from jax.sharding import PartitionSpec as P

score_temp = 0.05
rank_temp = 1.0
recall_depth = 5.0
loss_scale = 16.0
norm_eps = 1e-06


def inverse_rms(values):
    return lax.rsqrt(jnp.mean(values * values, axis=-1, keepdims=True) + norm_eps)


def normed_input(states, ff_gain):
    widened = states.astype(jnp.float32)
    return (widened * inverse_rms(widened) * ff_gain).astype(jnp.bfloat16)


def pooled_embedding(summed, tokens, out_gain, proj_weight):
    normed = summed * inverse_rms(summed) * out_gain
    token_mask = (tokens != 0).astype(jnp.float32)[:, :, None]
    pooled = jnp.sum(normed * token_mask, axis=1) / jnp.sum(token_mask, axis=1)
    projected = jnp.dot(pooled, proj_weight.astype(jnp.float32), precision=lax.Precision.HIGHEST)
    return projected * lax.rsqrt(jnp.sum(projected * projected, axis=-1, keepdims=True) + norm_eps)


def recall_loss(scores, valid_mask):
    margins = (scores[:, 1:] - scores[:, :1]) / score_temp
    soft_ranks = 1.0 + jnp.sum(jax.nn.sigmoid(margins) * valid_mask, axis=1)
    return loss_scale * jnp.sum(jax.nn.sigmoid((soft_ranks - recall_depth - 0.5) / rank_temp))


def contract(left, right):
    return lax.dot_general(
        left, right, (((0,), (0,)), ((), ())), preferred_element_type=jnp.float32
    )


def natural_order(gathered, segments, groups, per_device):
    model_width = gathered.shape[-1]
    shaped = gathered.reshape(segments, groups, per_device, model_width)
    return jnp.transpose(shaped, (1, 0, 2, 3)).reshape(-1, model_width)


def score_grads_of(scores, counts):
    slots = scores.shape[1] - 1
    valid_mask = (
        lax.broadcasted_iota(jnp.int32, (scores.shape[0], slots), 1) < counts[:, None]
    ).astype(jnp.float32)
    return jax.grad(recall_loss)(scores, valid_mask)


def body(
    query_states,
    passage_states,
    query_tokens,
    passage_tokens,
    ff_gains,
    out_gains,
    w_gate,
    w_up,
    w_down,
    w_proj,
    positive_ids,
    negative_ids,
    negative_counts,
):
    segments = lax.axis_size("segment")
    groups = lax.axis_size("dp")
    segment_index = lax.axis_index("segment")
    model_width = query_states.shape[-1]
    query_dev = query_states.shape[0] // segments
    passage_dev = passage_states.shape[0] // segments

    def forward_part(states, tower_index):
        normed = normed_input(states, ff_gains[tower_index]).reshape(-1, model_width)
        gate_pre = jnp.dot(normed, w_gate[tower_index], preferred_element_type=jnp.float32)
        up_pre = jnp.dot(normed, w_up[tower_index], preferred_element_type=jnp.float32)
        activated, gelu_back = jax.vjp(jax.nn.gelu, gate_pre)
        hidden = (activated * up_pre).astype(jnp.bfloat16)
        branch = jnp.dot(hidden, w_down[tower_index], preferred_element_type=jnp.float32).reshape(
            states.shape
        )
        return (normed, up_pre, activated, gelu_back, hidden, branch)

    def own_rows(values, per_device):
        return lax.dynamic_slice_in_dim(values, segment_index * per_device, per_device, 0)

    def head_of(tokens, tower_index):
        return lambda summed: pooled_embedding(
            summed, tokens, out_gains[tower_index], w_proj[tower_index]
        )

    query_parts = forward_part(query_states, 0)
    passage_parts = forward_part(passage_states, 1)
    query_block = query_parts[5].reshape(segments, -1, model_width)
    passage_block = passage_parts[5].reshape(segments, -1, model_width)
    query_size = query_block.shape[1]
    branch_sum = lax.psum_scatter(
        jnp.concatenate([query_block, passage_block], axis=1),
        "segment",
        scatter_dimension=0,
        tiled=True,
    )[0]
    query_branch = branch_sum[:query_size].reshape((query_dev,) + query_states.shape[1:])
    passage_branch = branch_sum[query_size:].reshape((passage_dev,) + passage_states.shape[1:])
    query_embed, query_back = jax.vjp(
        head_of(own_rows(query_tokens, query_dev), 0),
        own_rows(query_states, query_dev).astype(jnp.float32) + query_branch,
    )
    passage_embed, passage_back = jax.vjp(
        head_of(own_rows(passage_tokens, passage_dev), 1),
        own_rows(passage_states, passage_dev).astype(jnp.float32) + passage_branch,
    )
    query_round = query_embed.astype(jnp.bfloat16)
    passage_round = passage_embed.astype(jnp.bfloat16)
    id_radix = 256
    own_ids = jnp.concatenate(
        [own_rows(positive_ids, query_dev)[:, None], own_rows(negative_ids, query_dev)], axis=1
    )
    slots = own_ids.shape[1]
    own_meta = jnp.concatenate(
        [own_ids // id_radix, own_ids % id_radix, own_rows(negative_counts, query_dev)[:, None]],
        axis=1,
    ).astype(jnp.bfloat16)
    meta_width = own_meta.shape[1]
    meta_rows = -(-query_dev * meta_width // model_width)
    meta_flat = jnp.pad(
        own_meta.reshape(-1), (0, meta_rows * model_width - query_dev * meta_width)
    ).reshape(meta_rows, model_width)
    packed = jnp.concatenate([query_round, passage_round, meta_flat], axis=0)
    devices = groups * segments
    gathered = lax.all_gather(packed[:, None, :], ("dp", "segment"), axis=1, tiled=True)
    query_all = gathered[:query_dev].reshape(query_dev, devices, model_width)
    passage_all = gathered[query_dev : query_dev + passage_dev].reshape(
        passage_dev, devices, model_width
    )
    meta_all = (
        gathered[query_dev + passage_dev :]
        .transpose(1, 0, 2)
        .reshape(devices, -1)[:, : query_dev * meta_width]
        .reshape(devices, query_dev, meta_width)
        .transpose(1, 0, 2)
        .reshape(-1, meta_width)
        .astype(jnp.int32)
    )
    cand_ids = meta_all[:, :slots] * id_radix + meta_all[:, slots : 2 * slots]
    cand_all = (cand_ids % passage_dev) * devices + cand_ids // passage_dev
    counts_all = meta_all[:, 2 * slots]
    passage_total = passage_dev * devices
    all_scores = lax.dot_general(
        query_all, passage_all, (((2,), (2,)), ((), ())), preferred_element_type=jnp.float32
    ).reshape(query_dev * devices, passage_total)
    every_id = lax.broadcasted_iota(jnp.int32, (1, 1, passage_total), 2)
    scores = jnp.sum(
        jnp.where(cand_all[:, :, None] == every_id, all_scores[:, None, :], 0.0), axis=2
    )
    score_grads = score_grads_of(scores, counts_all)
    device_index = lax.axis_index("dp") * segments + segment_index
    own_cand = lax.dynamic_index_in_dim(
        cand_all.reshape(query_dev, devices, slots), device_index, 1, keepdims=False
    )
    own_grads = lax.dynamic_index_in_dim(
        score_grads.reshape(query_dev, devices, slots), device_index, 1, keepdims=False
    )
    query_coef = jnp.sum(
        jnp.where(own_cand[:, :, None] == every_id, own_grads[:, :, None], 0.0), axis=1
    )
    own_passages = (
        lax.broadcasted_iota(jnp.int32, (1, 1, passage_dev), 2) * devices + device_index
    )
    passage_coef = jnp.sum(
        jnp.where(cand_all[:, :, None] == own_passages, score_grads[:, :, None], 0.0), axis=1
    )
    query_grad = lax.dot_general(
        query_coef.reshape(query_dev, passage_dev, devices),
        passage_all.astype(jnp.float32),
        (((1, 2), (0, 1)), ((), ())),
        precision=lax.Precision.HIGHEST,
        preferred_element_type=jnp.float32,
    )
    passage_grad = lax.dot_general(
        passage_coef.reshape(query_dev, devices, passage_dev),
        query_all.astype(jnp.float32),
        (((0, 1), (0, 1)), ((), ())),
        precision=lax.Precision.HIGHEST,
        preferred_element_type=jnp.float32,
    )
    query_share = query_back(query_grad)[0].astype(jnp.bfloat16)
    passage_share = passage_back(passage_grad)[0].astype(jnp.bfloat16)
    share_rows = lax.all_gather(
        jnp.concatenate(
            [query_share.reshape(-1, model_width), passage_share.reshape(-1, model_width)], axis=0
        ),
        "segment",
        axis=0,
        tiled=False,
    )
    query_rows = share_rows[:, :query_size].reshape(query_states.shape)
    passage_rows = share_rows[:, query_size:].reshape(passage_states.shape)

    def backward_part(tower_parts, row_grads, tower_index):
        normed, up_pre, activated, gelu_back, hidden, branch = tower_parts
        flat_grad = row_grads.reshape(-1, model_width)
        hidden_grad = lax.dot_general(
            flat_grad,
            w_down[tower_index],
            (((1,), (1,)), ((), ())),
            preferred_element_type=jnp.float32,
        )
        gate_grad = gelu_back(hidden_grad * up_pre)[0].astype(jnp.bfloat16)
        up_grad = (hidden_grad * activated).astype(jnp.bfloat16)
        return (normed, gate_grad, up_grad, hidden, flat_grad)

    towers_back = (
        backward_part(query_parts, query_rows, 0),
        backward_part(passage_parts, passage_rows, 1),
    )

    def weight_terms():
        matrices = [[], [], []]
        for normed, gate_grad, up_grad, hidden, flat_grad in towers_back:
            matrices[0].append(contract(normed, gate_grad))
            matrices[1].append(contract(normed, up_grad))
            matrices[2].append(contract(flat_grad, hidden))
        return jnp.stack([jnp.stack(pieces, axis=1) for pieces in matrices], axis=1)

    summed_grads = lax.psum_scatter(weight_terms(), "dp", scatter_dimension=0, tiled=True)
    grad_gate = jnp.transpose(summed_grads[:, 0], (1, 0, 2))
    grad_up = jnp.transpose(summed_grads[:, 1], (1, 0, 2))
    grad_down = jnp.transpose(summed_grads[:, 2], (1, 2, 0))
    return (grad_gate, grad_up, grad_down)


def solution(mesh):
    return jax.shard_map(
        body,
        mesh=mesh,
        in_specs=(
            P("dp", None, None),
            P("dp", None, None),
            P("dp", None),
            P("dp", None),
            P(),
            P(),
            P(None, None, "segment"),
            P(None, None, "segment"),
            P(None, "segment", None),
            P(),
            P("dp"),
            P("dp", None),
            P("dp"),
        ),
        out_specs=(P(None, "dp", "segment"), P(None, "dp", "segment"), P(None, "segment", "dp")),
        check_vma=False,
    )
```

```python
import jax
import jax.numpy as jnp
from jax import lax
from jax.sharding import PartitionSpec as P

score_temp = 0.05
rank_temp = 1.0
recall_depth = 5.0
loss_scale = 16.0
norm_eps = 1e-06


def inverse_rms(values):
    return lax.rsqrt(jnp.mean(values * values, axis=-1, keepdims=True) + norm_eps)


def normed_input(states, ff_gain):
    widened = states.astype(jnp.float32)
    return (widened * inverse_rms(widened) * ff_gain).astype(jnp.bfloat16)


def pooled_embedding(summed, tokens, out_gain, proj_weight):
    normed = summed * inverse_rms(summed) * out_gain
    token_mask = (tokens != 0).astype(jnp.float32)[:, :, None]
    pooled = jnp.sum(normed * token_mask, axis=1) / jnp.sum(token_mask, axis=1)
    projected = jnp.dot(pooled, proj_weight.astype(jnp.float32), precision=lax.Precision.HIGHEST)
    return projected * lax.rsqrt(jnp.sum(projected * projected, axis=-1, keepdims=True) + norm_eps)


def recall_loss(scores, valid_mask):
    margins = (scores[:, 1:] - scores[:, :1]) / score_temp
    soft_ranks = 1.0 + jnp.sum(jax.nn.sigmoid(margins) * valid_mask, axis=1)
    return loss_scale * jnp.sum(jax.nn.sigmoid((soft_ranks - recall_depth - 0.5) / rank_temp))


def contract(left, right):
    return lax.dot_general(
        left, right, (((0,), (0,)), ((), ())), preferred_element_type=jnp.float32
    )


def natural_order(gathered, segments, groups, per_device):
    model_width = gathered.shape[-1]
    shaped = gathered.reshape(segments, groups, per_device, model_width)
    return jnp.transpose(shaped, (1, 0, 2, 3)).reshape(-1, model_width)


def score_grads_of(scores, counts):
    slots = scores.shape[1] - 1
    valid_mask = (
        lax.broadcasted_iota(jnp.int32, (scores.shape[0], slots), 1) < counts[:, None]
    ).astype(jnp.float32)
    return jax.grad(recall_loss)(scores, valid_mask)


def body(
    query_states,
    passage_states,
    query_tokens,
    passage_tokens,
    ff_gains,
    out_gains,
    w_gate,
    w_up,
    w_down,
    w_proj,
    positive_ids,
    negative_ids,
    negative_counts,
):
    segments = lax.axis_size("segment")
    groups = lax.axis_size("dp")
    segment_index = lax.axis_index("segment")
    model_width = query_states.shape[-1]
    query_dev = query_states.shape[0] // segments
    passage_dev = passage_states.shape[0] // segments

    def forward_part(states, tower_index):
        normed = normed_input(states, ff_gains[tower_index]).reshape(-1, model_width)
        gate_pre = jnp.dot(normed, w_gate[tower_index], preferred_element_type=jnp.float32)
        up_pre = jnp.dot(normed, w_up[tower_index], preferred_element_type=jnp.float32)
        activated, gelu_back = jax.vjp(jax.nn.gelu, gate_pre)
        hidden = (activated * up_pre).astype(jnp.bfloat16)
        branch = jnp.dot(hidden, w_down[tower_index], preferred_element_type=jnp.float32).reshape(
            states.shape
        )
        return (normed, up_pre, activated, gelu_back, hidden, branch)

    def own_rows(values, per_device):
        return lax.dynamic_slice_in_dim(values, segment_index * per_device, per_device, 0)

    def head_of(tokens, tower_index):
        return lambda summed: pooled_embedding(
            summed, tokens, out_gains[tower_index], w_proj[tower_index]
        )

    query_parts = forward_part(query_states, 0)
    passage_parts = forward_part(passage_states, 1)
    query_block = query_parts[5].reshape(segments, -1, model_width)
    passage_block = passage_parts[5].reshape(segments, -1, model_width)
    query_size = query_block.shape[1]
    branch_sum = lax.psum_scatter(
        jnp.concatenate([query_block, passage_block], axis=1),
        "segment",
        scatter_dimension=0,
        tiled=True,
    )[0]
    query_branch = branch_sum[:query_size].reshape((query_dev,) + query_states.shape[1:])
    passage_branch = branch_sum[query_size:].reshape((passage_dev,) + passage_states.shape[1:])
    query_embed, query_back = jax.vjp(
        head_of(own_rows(query_tokens, query_dev), 0),
        own_rows(query_states, query_dev).astype(jnp.float32) + query_branch,
    )
    passage_embed, passage_back = jax.vjp(
        head_of(own_rows(passage_tokens, passage_dev), 1),
        own_rows(passage_states, passage_dev).astype(jnp.float32) + passage_branch,
    )
    query_round = query_embed.astype(jnp.bfloat16)
    passage_round = passage_embed.astype(jnp.bfloat16)
    id_radix = 256
    own_ids = jnp.concatenate(
        [own_rows(positive_ids, query_dev)[:, None], own_rows(negative_ids, query_dev)], axis=1
    )
    slots = own_ids.shape[1]
    own_meta = jnp.concatenate(
        [own_ids // id_radix, own_ids % id_radix, own_rows(negative_counts, query_dev)[:, None]],
        axis=1,
    ).astype(jnp.bfloat16)
    meta_width = own_meta.shape[1]
    meta_rows = -(-query_dev * meta_width // model_width)
    meta_flat = jnp.pad(
        own_meta.reshape(-1), (0, meta_rows * model_width - query_dev * meta_width)
    ).reshape(meta_rows, model_width)
    packed = jnp.concatenate([query_round, passage_round, meta_flat], axis=0)
    devices = groups * segments
    gathered = lax.all_gather(packed[:, None, :], ("dp", "segment"), axis=1, tiled=True)
    query_all = gathered[:query_dev].reshape(query_dev, devices, model_width)
    passage_all = gathered[query_dev : query_dev + passage_dev].reshape(
        passage_dev, devices, model_width
    )
    meta_all = (
        gathered[query_dev + passage_dev :]
        .transpose(1, 0, 2)
        .reshape(devices, -1)[:, : query_dev * meta_width]
        .reshape(devices, query_dev, meta_width)
        .transpose(1, 0, 2)
        .reshape(-1, meta_width)
        .astype(jnp.int32)
    )
    cand_ids = meta_all[:, :slots] * id_radix + meta_all[:, slots : 2 * slots]
    cand_all = (cand_ids % passage_dev) * devices + cand_ids // passage_dev
    counts_all = meta_all[:, 2 * slots]
    passage_total = passage_dev * devices
    all_scores = lax.dot_general(
        query_all, passage_all, (((2,), (2,)), ((), ())), preferred_element_type=jnp.float32
    ).reshape(query_dev * devices, passage_total)
    every_id = lax.broadcasted_iota(jnp.int32, (1, 1, passage_total), 2)
    device_index = lax.axis_index("dp") * segments + segment_index
    own_cand = (own_ids % passage_dev) * devices + own_ids // passage_dev
    own_scores = jnp.sum(
        jnp.where(
            own_cand[:, :, None] == every_id,
            lax.dot_general(
                query_round,
                passage_all,
                (((1,), (2,)), ((), ())),
                preferred_element_type=jnp.float32,
            ).reshape(query_dev, 1, passage_total),
            0.0,
        ),
        axis=2,
    )
    own_grads = score_grads_of(own_scores, own_rows(negative_counts, query_dev))
    query_coef = jnp.sum(
        jnp.where(own_cand[:, :, None] == every_id, own_grads[:, :, None], 0.0), axis=1
    )
    query_grad = lax.dot_general(
        query_coef.reshape(query_dev, passage_dev, devices),
        passage_all.astype(jnp.float32),
        (((1, 2), (0, 1)), ((), ())),
        precision=lax.Precision.HIGHEST,
        preferred_element_type=jnp.float32,
    )
    query_share = query_back(query_grad)[0].astype(jnp.bfloat16)
    query_rows = lax.all_gather(query_share, "segment", axis=0, tiled=True)
    scores = jnp.sum(
        jnp.where(cand_all[:, :, None] == every_id, all_scores[:, None, :], 0.0), axis=2
    )
    score_grads = score_grads_of(scores, counts_all)
    own_passages = (
        lax.broadcasted_iota(jnp.int32, (1, 1, passage_dev), 2) * devices + device_index
    )
    passage_coef = jnp.sum(
        jnp.where(cand_all[:, :, None] == own_passages, score_grads[:, :, None], 0.0), axis=1
    )
    passage_grad = lax.dot_general(
        passage_coef.reshape(query_dev, devices, passage_dev),
        query_all.astype(jnp.float32),
        (((0, 1), (0, 1)), ((), ())),
        precision=lax.Precision.HIGHEST,
        preferred_element_type=jnp.float32,
    )
    passage_share = passage_back(passage_grad)[0].astype(jnp.bfloat16)
    passage_rows = lax.all_gather(passage_share, "segment", axis=0, tiled=True)

    def backward_part(tower_parts, row_grads, tower_index):
        normed, up_pre, activated, gelu_back, hidden, branch = tower_parts
        flat_grad = row_grads.reshape(-1, model_width)
        hidden_grad = lax.dot_general(
            flat_grad,
            w_down[tower_index],
            (((1,), (1,)), ((), ())),
            preferred_element_type=jnp.float32,
        )
        gate_grad = gelu_back(hidden_grad * up_pre)[0].astype(jnp.bfloat16)
        up_grad = (hidden_grad * activated).astype(jnp.bfloat16)
        return (normed, gate_grad, up_grad, hidden, flat_grad)

    towers_back = (
        backward_part(query_parts, query_rows, 0),
        backward_part(passage_parts, passage_rows, 1),
    )

    def weight_terms():
        matrices = [[], [], []]
        for normed, gate_grad, up_grad, hidden, flat_grad in towers_back:
            matrices[0].append(contract(normed, gate_grad))
            matrices[1].append(contract(normed, up_grad))
            matrices[2].append(contract(flat_grad, hidden))
        return jnp.stack([jnp.stack(pieces, axis=1) for pieces in matrices], axis=1)

    summed_grads = lax.psum_scatter(weight_terms(), "dp", scatter_dimension=0, tiled=True)
    grad_gate = jnp.transpose(summed_grads[:, 0], (1, 0, 2))
    grad_up = jnp.transpose(summed_grads[:, 1], (1, 0, 2))
    grad_down = jnp.transpose(summed_grads[:, 2], (1, 2, 0))
    return (grad_gate, grad_up, grad_down)


def solution(mesh):
    return jax.shard_map(
        body,
        mesh=mesh,
        in_specs=(
            P("dp", None, None),
            P("dp", None, None),
            P("dp", None),
            P("dp", None),
            P(),
            P(),
            P(None, None, "segment"),
            P(None, None, "segment"),
            P(None, "segment", None),
            P(),
            P("dp"),
            P("dp", None),
            P("dp"),
        ),
        out_specs=(P(None, "dp", "segment"), P(None, "dp", "segment"), P(None, "segment", "dp")),
        check_vma=False,
    )
```

```python
import jax
import jax.numpy as jnp
from jax import lax
from jax.sharding import PartitionSpec as P

score_temp = 0.05
rank_temp = 1.0
recall_depth = 5.0
loss_scale = 16.0
norm_eps = 1e-06


def inverse_rms(values):
    return lax.rsqrt(jnp.mean(values * values, axis=-1, keepdims=True) + norm_eps)


def normed_input(states, ff_gain):
    widened = states.astype(jnp.float32)
    return (widened * inverse_rms(widened) * ff_gain).astype(jnp.bfloat16)


def pooled_embedding(summed, tokens, out_gain, proj_weight):
    normed = summed * inverse_rms(summed) * out_gain
    token_mask = (tokens != 0).astype(jnp.float32)[:, :, None]
    pooled = jnp.sum(normed * token_mask, axis=1) / jnp.sum(token_mask, axis=1)
    projected = jnp.dot(pooled, proj_weight.astype(jnp.float32), precision=lax.Precision.HIGHEST)
    return projected * lax.rsqrt(jnp.sum(projected * projected, axis=-1, keepdims=True) + norm_eps)


def recall_loss(scores, valid_mask):
    margins = (scores[:, 1:] - scores[:, :1]) / score_temp
    soft_ranks = 1.0 + jnp.sum(jax.nn.sigmoid(margins) * valid_mask, axis=1)
    return loss_scale * jnp.sum(jax.nn.sigmoid((soft_ranks - recall_depth - 0.5) / rank_temp))


def contract(left, right):
    return lax.dot_general(
        left, right, (((0,), (0,)), ((), ())), preferred_element_type=jnp.float32
    )


def natural_order(gathered, segments, groups, per_device):
    model_width = gathered.shape[-1]
    shaped = gathered.reshape(segments, groups, per_device, model_width)
    return jnp.transpose(shaped, (1, 0, 2, 3)).reshape(-1, model_width)


def score_grads_of(scores, counts):
    slots = scores.shape[1] - 1
    valid_mask = (
        lax.broadcasted_iota(jnp.int32, (scores.shape[0], slots), 1) < counts[:, None]
    ).astype(jnp.float32)
    return jax.grad(recall_loss)(scores, valid_mask)


def body(
    query_states,
    passage_states,
    query_tokens,
    passage_tokens,
    ff_gains,
    out_gains,
    w_gate,
    w_up,
    w_down,
    w_proj,
    positive_ids,
    negative_ids,
    negative_counts,
):
    segments = lax.axis_size("segment")
    groups = lax.axis_size("dp")
    segment_index = lax.axis_index("segment")
    model_width = query_states.shape[-1]
    query_dev = query_states.shape[0] // segments
    passage_dev = passage_states.shape[0] // segments

    def forward_part(states, tower_index):
        normed = normed_input(states, ff_gains[tower_index]).reshape(-1, model_width)
        gate_pre = jnp.dot(normed, w_gate[tower_index], preferred_element_type=jnp.float32)
        up_pre = jnp.dot(normed, w_up[tower_index], preferred_element_type=jnp.float32)
        activated, gelu_back = jax.vjp(jax.nn.gelu, gate_pre)
        hidden = (activated * up_pre).astype(jnp.bfloat16)
        branch = jnp.dot(hidden, w_down[tower_index], preferred_element_type=jnp.float32).reshape(
            states.shape
        )
        return (normed, up_pre, activated, gelu_back, hidden, branch)

    def own_rows(values, per_device):
        return lax.dynamic_slice_in_dim(values, segment_index * per_device, per_device, 0)

    def head_of(tokens, tower_index):
        return lambda summed: pooled_embedding(
            summed, tokens, out_gains[tower_index], w_proj[tower_index]
        )

    query_parts = forward_part(query_states, 0)
    passage_parts = forward_part(passage_states, 1)
    query_block = query_parts[5].reshape(segments, -1, model_width)
    passage_block = passage_parts[5].reshape(segments, -1, model_width)
    query_size = query_block.shape[1]
    branch_sum = lax.psum_scatter(
        jnp.concatenate([query_block, passage_block], axis=1),
        "segment",
        scatter_dimension=0,
        tiled=True,
    )[0]
    query_branch = branch_sum[:query_size].reshape((query_dev,) + query_states.shape[1:])
    passage_branch = branch_sum[query_size:].reshape((passage_dev,) + passage_states.shape[1:])
    query_embed, query_back = jax.vjp(
        head_of(own_rows(query_tokens, query_dev), 0),
        own_rows(query_states, query_dev).astype(jnp.float32) + query_branch,
    )
    passage_embed, passage_back = jax.vjp(
        head_of(own_rows(passage_tokens, passage_dev), 1),
        own_rows(passage_states, passage_dev).astype(jnp.float32) + passage_branch,
    )
    query_round = query_embed.astype(jnp.bfloat16)
    passage_round = passage_embed.astype(jnp.bfloat16)
    id_radix = 256
    own_ids = jnp.concatenate(
        [own_rows(positive_ids, query_dev)[:, None], own_rows(negative_ids, query_dev)], axis=1
    )
    slots = own_ids.shape[1]
    own_meta = jnp.concatenate(
        [own_ids // id_radix, own_ids % id_radix, own_rows(negative_counts, query_dev)[:, None]],
        axis=1,
    ).astype(jnp.bfloat16)
    meta_width = own_meta.shape[1]
    meta_rows = -(-query_dev * meta_width // model_width)
    meta_flat = jnp.pad(
        own_meta.reshape(-1), (0, meta_rows * model_width - query_dev * meta_width)
    ).reshape(meta_rows, model_width)
    packed = jnp.concatenate([query_round, passage_round, meta_flat], axis=0)
    devices = groups * segments
    gathered = lax.all_gather(packed[:, None, :], ("dp", "segment"), axis=1, tiled=True)
    query_all = gathered[:query_dev].reshape(query_dev, devices, model_width)
    passage_all = gathered[query_dev : query_dev + passage_dev].reshape(
        passage_dev, devices, model_width
    )
    meta_all = (
        gathered[query_dev + passage_dev :]
        .transpose(1, 0, 2)
        .reshape(devices, -1)[:, : query_dev * meta_width]
        .reshape(devices, query_dev, meta_width)
        .transpose(1, 0, 2)
        .reshape(-1, meta_width)
        .astype(jnp.int32)
    )
    cand_ids = meta_all[:, :slots] * id_radix + meta_all[:, slots : 2 * slots]
    cand_all = (cand_ids % passage_dev) * devices + cand_ids // passage_dev
    counts_all = meta_all[:, 2 * slots]
    passage_total = passage_dev * devices
    all_scores = lax.dot_general(
        gathered.reshape(-1, devices, model_width),
        passage_all,
        (((2,), (2,)), ((), ())),
        preferred_element_type=jnp.float32,
    )[:query_dev].reshape(query_dev * devices, passage_total)
    every_id = lax.broadcasted_iota(jnp.int32, (1, 1, passage_total), 2)
    scores = jnp.sum(
        jnp.where(cand_all[:, :, None] == every_id, all_scores[:, None, :], 0.0), axis=2
    )
    score_grads = score_grads_of(scores, counts_all)
    device_index = lax.axis_index("dp") * segments + segment_index
    own_cand = lax.dynamic_index_in_dim(
        cand_all.reshape(query_dev, devices, slots), device_index, 1, keepdims=False
    )
    own_grads = lax.dynamic_index_in_dim(
        score_grads.reshape(query_dev, devices, slots), device_index, 1, keepdims=False
    )
    query_coef = jnp.sum(
        jnp.where(own_cand[:, :, None] == every_id, own_grads[:, :, None], 0.0), axis=1
    )
    own_passages = (
        lax.broadcasted_iota(jnp.int32, (1, 1, passage_dev), 2) * devices + device_index
    )
    passage_coef = jnp.sum(
        jnp.where(cand_all[:, :, None] == own_passages, score_grads[:, :, None], 0.0), axis=1
    )
    query_grad = lax.dot_general(
        query_coef.reshape(query_dev, passage_dev, devices),
        passage_all.astype(jnp.float32),
        (((1, 2), (0, 1)), ((), ())),
        precision=lax.Precision.HIGHEST,
        preferred_element_type=jnp.float32,
    )
    slot_count = gathered.shape[0]
    passage_grad = lax.dot_general(
        jnp.pad(
            passage_coef.reshape(query_dev, devices, passage_dev),
            ((0, slot_count - query_dev), (0, 0), (0, 0)),
        ),
        gathered.reshape(-1, devices, model_width).astype(jnp.float32),
        (((0, 1), (0, 1)), ((), ())),
        precision=lax.Precision.HIGHEST,
        preferred_element_type=jnp.float32,
    )
    query_share = query_back(query_grad)[0].astype(jnp.bfloat16)
    passage_share = passage_back(passage_grad)[0].astype(jnp.bfloat16)
    share_rows = lax.all_gather(
        jnp.concatenate(
            [query_share.reshape(-1, model_width), passage_share.reshape(-1, model_width)], axis=0
        ),
        "segment",
        axis=0,
        tiled=False,
    )
    query_rows = share_rows[:, :query_size].reshape(query_states.shape)
    passage_rows = share_rows[:, query_size:].reshape(passage_states.shape)

    def backward_part(tower_parts, row_grads, tower_index):
        normed, up_pre, activated, gelu_back, hidden, branch = tower_parts
        flat_grad = row_grads.reshape(-1, model_width)
        hidden_grad = lax.dot_general(
            flat_grad,
            w_down[tower_index],
            (((1,), (1,)), ((), ())),
            preferred_element_type=jnp.float32,
        )
        gate_grad = gelu_back(hidden_grad * up_pre)[0].astype(jnp.bfloat16)
        up_grad = (hidden_grad * activated).astype(jnp.bfloat16)
        return (normed, gate_grad, up_grad, hidden, flat_grad)

    towers_back = (
        backward_part(query_parts, query_rows, 0),
        backward_part(passage_parts, passage_rows, 1),
    )

    def weight_terms():
        matrices = [[], [], []]
        for normed, gate_grad, up_grad, hidden, flat_grad in towers_back:
            matrices[0].append(contract(normed, gate_grad))
            matrices[1].append(contract(normed, up_grad))
            matrices[2].append(contract(flat_grad, hidden))
        return jnp.stack([jnp.stack(pieces, axis=1) for pieces in matrices], axis=1)

    summed_grads = lax.psum_scatter(weight_terms(), "dp", scatter_dimension=0, tiled=True)
    grad_gate = jnp.transpose(summed_grads[:, 0], (1, 0, 2))
    grad_up = jnp.transpose(summed_grads[:, 1], (1, 0, 2))
    grad_down = jnp.transpose(summed_grads[:, 2], (1, 2, 0))
    return (grad_gate, grad_up, grad_down)


def solution(mesh):
    return jax.shard_map(
        body,
        mesh=mesh,
        in_specs=(
            P("dp", None, None),
            P("dp", None, None),
            P("dp", None),
            P("dp", None),
            P(),
            P(),
            P(None, None, "segment"),
            P(None, None, "segment"),
            P(None, "segment", None),
            P(),
            P("dp"),
            P("dp", None),
            P("dp"),
        ),
        out_specs=(P(None, "dp", "segment"), P(None, "dp", "segment"), P(None, "segment", "dp")),
        check_vma=False,
    )
```
